256 devices in a mesh: grp: 4 (over y), ex: 8 (over x, core), tp: 8 (over z).
Axes of the slice: x: 4, y: 4, z: 8, core: 2. Of those that a mesh axis runs over, the one named last changes fastest.
Arguments:
- residual: bfloat16 [512, 2, 6144], P(('grp', 'ex'), None, 'tp'), may hold values from -34 to 34
- query_new: bfloat16 [512, 2, 6144], P(('grp', 'ex'), None, 'tp'), may hold values from -5 to 5
- key_new: bfloat16 [512, 2, 1024], P(('grp', 'ex'), None, 'tp'), may hold values from -8 to 8
- value_new: bfloat16 [512, 2, 1024], P(('grp', 'ex'), None, 'tp'), may hold values from -12 to 12
- key_cache: bfloat16 [512, 8, 512, 128], P(('grp', 'ex'), 'tp'), may hold values from -5 to 5
- value_cache: bfloat16 [512, 8, 512, 128], P(('grp', 'ex'), 'tp'), may hold values from -12 to 12
- lengths: int32 [512], P(('grp', 'ex')), may hold values from 128 to 512, as said below
- norm_gain: bfloat16 [6144], P('tp'), may hold values from 0.099609375 to 1.8984375
- router: float32 [6144, 8], P('tp'), may hold values from -0.078125 to 0.078125
- routes: int32 [512, 2, 2], P(('grp', 'ex')), may hold values from 0 to 7, all different within a row; in each aligned block of 32 rows (0 to 31, 32 to 63, ..., all dimensions but the last counted through in order) at most 16 rows name the same one
- w_gate: bfloat16 [8, 6144, 8192], P('ex', None, ('grp', 'tp')), may hold values from -0.078125 to 0.078125
- w_up: bfloat16 [8, 6144, 8192], P('ex', None, ('grp', 'tp')), may hold values from -0.078125 to 0.078125
- w_down: bfloat16 [8, 8192, 6144], P('ex', ('grp', 'tp')), may hold values from -0.125 to 0.125
Outputs:
- attended: bfloat16 [512, 2, 6144], P(('grp', 'ex'), None, 'tp')
- expert_mix: bfloat16 [512, 2, 6144], P(('grp', 'ex'), None, 'tp')
The draws below stay inside these ranges and needn't reach their ends.
Inputs may be any that keep to these rules, and one draw needn't show every extreme that they name: `routes`: over the rows of one device (aligned blocks of 32 rows, environments then steps) no expert is named more than 16 times, and in some blocks one is named exactly 16 times; a row's two experts differ. `lengths`: some environment's cache is full.
All inputs are finite; a program needn't handle non-finite values.
Results may differ from the reference program's by a relative error of at most 0.023.
Values may be sent and summed in bfloat16 or wider, within the bound.
No kernel may reach another device: no remote copies, remote signals or barrier semaphores. Data moves between devices by JAX's collectives and lax.ppermute only.
A program may use at most 128 MiB of HBM per device.

```python
import math
import jax
import jax.numpy as jnp
import numpy as np
from jax import lax

D = 6144
H = 48
KVH = 8
HD = 128
EXPERTS = 8
TOPK = 2
FF = 8192
CTX = 512
STEPS = 2
ENV_DEV = 16
ENVS = 512
CAP = 16


def draw_key_cache(key, part):
    noise_key = jax.random.fold_in(key, 11)
    drawn = jnp.clip(jax.random.normal(noise_key, (ENVS, KVH, CTX, HD), jnp.float32), -4.0, 4.0)
    return drawn.astype(jnp.bfloat16)


def draw_query_new(key, part):
    noise_key = jax.random.fold_in(key, 12)
    full_shape = (ENVS, STEPS, KVH, H // KVH, HD)
    drawn = jnp.clip(jax.random.normal(noise_key, full_shape, jnp.float32), -4.0, 4.0)
    return drawn.reshape(ENVS, STEPS, D).astype(jnp.bfloat16)


def draw_residual(key, part):
    row_key, column_key, noise_key = jax.random.split(jax.random.fold_in(key, 13), 3)
    row_scale = jnp.exp(jax.random.uniform(row_key, (ENVS, STEPS, 1), jnp.float32, 0.0, math.log(10.0)))
    column_scale = 10.0 ** (jnp.arange(D, dtype=jnp.float32) / D) * jnp.exp(jax.random.uniform(column_key, (D,), jnp.float32, -0.3, 0.3))
    drawn = jnp.clip(jax.random.normal(noise_key, (ENVS, STEPS, D), jnp.float32), -4.0, 4.0)
    return (0.05 * drawn * row_scale * column_scale).astype(jnp.bfloat16)


def draw_lengths(key, part):
    fill_key, pick_key = jax.random.split(jax.random.fold_in(key, 14))
    drawn = jax.random.randint(fill_key, (ENVS,), CTX // 4, CTX + 1)
    longest = jax.random.randint(pick_key, (), 0, ENVS)
    return jnp.where(jnp.arange(ENVS) == longest, CTX, drawn).astype(jnp.int32)


def strengthened(values, own_key, source, target, blocks, factor):
    owner, partner = [(jnp.arange(values.shape[dim]) // (values.shape[dim] // blocks)).reshape([-1 if axis == dim else 1 for axis in range(values.ndim)]) for dim in (source, target)]
    chosen = jax.random.permutation(own_key, blocks)[partner]
    strong = (owner == chosen) | (owner == (partner + blocks // 2) % blocks)
    return jnp.where(strong, factor * values, values)


def block_scale(stream_key, shape, cuts, smallest, high):
    factor_of = 1.0
    for position, parts in cuts:
        heights = jax.random.uniform(jax.random.fold_in(jax.random.fold_in(stream_key, 6), position), (parts,), jnp.float32, smallest / len(cuts), high / len(cuts))
        factor_of = factor_of * jnp.repeat(jnp.exp(heights), shape[position] // parts).reshape((-1,) + (1,) * (len(shape) - 1 - position))
    return factor_of


def deal_out(key, own, number, rows, amount, top, bound, skew):
    ranking = jax.random.permutation(key, amount)
    heavy_load, usual = shares(amount, rows * top, bound, skew, True), shares(amount, rows * top, bound, skew, False)
    places = jnp.arange(amount)

    def named(tallies, rotation):
        used = int((tallies > 0).sum())
        fixed = max(1, used // 4)
        moved = fixed + (places - fixed + rotation * (used - fixed)) % max(1, amount - fixed)
        return jnp.zeros((amount,), jnp.int32).at[ranking[jnp.where(places < fixed, places, moved)]].set(jnp.asarray(tallies, jnp.int32))

    tallies = jnp.where(number % 4 == 0, named(heavy_load, number // 4), named(usual, number - number // 4 - 1))
    mixed = jax.random.permutation(jax.random.fold_in(own, 3), amount)
    donor, taker = mixed[0:amount // 2 * 2:2], mixed[1:amount // 2 * 2:2]
    room = jnp.minimum(tallies[donor] - 1, bound - tallies[taker]) // 2
    room = jnp.where((donor == ranking[0]) | (taker == ranking[0]) | (tallies[taker] == 0), 0, jnp.maximum(room, 0))
    moved = jax.random.randint(jax.random.fold_in(own, 4), (amount // 2,), 0, 1 << 20) % (room + 1)
    tallies = tallies.at[donor].add(-moved).at[taker].add(moved)
    labels = jnp.searchsorted(jnp.cumsum(tallies), jnp.arange(rows * top), side="right").astype(jnp.int32)
    listing = labels.reshape(top, rows).T
    listing = listing[jax.random.permutation(jax.random.fold_in(own, 1), rows)]
    rotation = jax.random.randint(jax.random.fold_in(own, 2), (rows, 1), 0, top)
    return jnp.take_along_axis(listing, (jnp.arange(top)[None, :] + rotation) % top, axis=1)


def shares(count, total, bound, skew, full):
    portions = [(1 << 20) // math.isqrt(standing ** skew) + 1 for standing in range(1, count + 1)]
    largest = bound if full else min(bound, max(-(-total // count), total * portions[0] // sum(portions)))
    least = 1 if total - largest >= count - 1 else 0
    holding, rest = [largest] + [least] * (count - 1), total - largest - least * (count - 1)
    while rest > 0:
        movable = [i for i in range(1, count) if holding[i] < largest] or [i for i in range(1, count) if holding[i] < bound]
        whole, remaining = sum([portions[i] for i in movable]), rest
        for i in movable:
            more = min(bound - holding[i], max(1, remaining * portions[i] // whole), rest)
            holding[i] = holding[i] + more
            rest = rest - more
    return np.array(holding)


def bell_draw(key, dims, spread, most, cuts=(), kind=jnp.bfloat16):
    gain = block_scale(key, dims, cuts, -0.22, 0.18) if cuts else 1.0
    entries = jax.random.normal(key, dims, jnp.float32) * spread * gain
    return jnp.minimum(jnp.maximum(entries, -most), most).astype(kind)


def bell_draw_with(rng, shape, scale, most, pieces, heavy, held_as=jnp.bfloat16):
    values = scale * jax.random.normal(rng, shape, jnp.float32)
    if pieces:
        values = values * block_scale(rng, shape, pieces, -0.22, 0.18)
    return jnp.clip(strengthened(values, jax.random.fold_in(rng, 3), *heavy), -most, most).astype(held_as)


def setup_inputs(seed: int = 0) -> dict:
    arg_keys = jax.random.split(jax.random.key(seed), 14)
    residual = draw_residual(jax.random.fold_in(arg_keys[13], 71), 0)
    query_new = draw_query_new(jax.random.fold_in(arg_keys[13], 71), 0)
    key_new = bell_draw(arg_keys[2], (ENVS, STEPS, KVH * HD), 2.0, 8.0, ((0, 32), (2, 8)))
    value_new = bell_draw(arg_keys[3], (ENVS, STEPS, KVH * HD), 3.0, 12.0, ((0, 32), (2, 8)))
    key_cache = draw_key_cache(jax.random.fold_in(arg_keys[13], 71), 0)
    value_cache = bell_draw(arg_keys[5], (ENVS, KVH, CTX, HD), 3.0, 12.0, ((0, 32), (1, 8)))
    lengths = draw_lengths(jax.random.fold_in(arg_keys[13], 71), 0)
    norm_gain = jnp.clip(1.0 + 0.18 * jax.random.normal(arg_keys[7], (D,), jnp.float32), 0.099609375, 1.8984375).astype(jnp.bfloat16)
    router = bell_draw(arg_keys[8], (D, EXPERTS), D ** -0.5, 0.078125, ((0, 8),), jnp.float32)
    routes_keys = jax.random.split(jax.random.fold_in(arg_keys[9], 1), ENVS * STEPS // (ENV_DEV * STEPS))
    routes_turns = jax.random.permutation(jax.random.fold_in(arg_keys[9], 3), ENVS * STEPS // (ENV_DEV * STEPS))
    routes = jax.vmap(lambda own, number: deal_out(jax.random.fold_in(arg_keys[9], 2), own, number, ENV_DEV * STEPS, EXPERTS, TOPK, CAP, 2))(routes_keys, routes_turns).reshape((ENVS, STEPS, TOPK))
    w_gate = bell_draw(arg_keys[10], (EXPERTS, D, FF), D ** -0.5, 0.078125, ((0, 8), (2, 32)))
    w_up = bell_draw(arg_keys[11], (EXPERTS, D, FF), D ** -0.5, 0.078125, ((0, 8), (2, 32)))
    w_down = bell_draw_with(arg_keys[12], (EXPERTS, FF, D), FF ** -0.5, 0.125, ((0, 8), (1, 32)), (1, 2, 32, 2.75))
    return {"residual": residual, "query_new": query_new, "key_new": key_new, "value_new": value_new, "key_cache": key_cache, "value_cache": value_cache, "lengths": lengths, "norm_gain": norm_gain, "router": router, "routes": routes, "w_gate": w_gate, "w_up": w_up, "w_down": w_down}


def attend(query_new, key_new, value_new, key_cache, value_cache, lengths):
    env_count, step_count, feature_count = query_new.shape
    kv_count = key_cache.shape[1]
    context = key_cache.shape[2]
    head_dim = key_cache.shape[3]
    group_size = feature_count // (kv_count * head_dim)
    queries = query_new.astype(jnp.float32).reshape(env_count, step_count, kv_count, group_size, head_dim)
    keys_now = key_new.astype(jnp.float32).reshape(env_count, step_count, kv_count, head_dim)
    values_now = value_new.astype(jnp.float32).reshape(env_count, step_count, kv_count, head_dim)
    score_scale = head_dim ** (-0.5)
    cached = jnp.einsum('eskgd,ekcd->eskgc', queries, key_cache.astype(jnp.float32)) * score_scale
    fresh_scores = jnp.einsum('eskgd,etkd->eskgt', queries, keys_now) * score_scale
    valid_mask = (lax.broadcasted_iota(jnp.int32, (env_count, context), 1) < lengths[:, None].astype(jnp.int32))[:, None, None, None, :]
    causal = (lax.broadcasted_iota(jnp.int32, (step_count, step_count), 1) <= lax.broadcasted_iota(jnp.int32, (step_count, step_count), 0))[None, :, None, None, :]
    cached = jnp.where(valid_mask, cached, -1e+30)
    fresh_scores = jnp.where(causal, fresh_scores, -1e+30)
    row_top = jnp.maximum(lax.optimization_barrier(jnp.max(cached, -1)), lax.optimization_barrier(jnp.max(fresh_scores, -1)))[..., None]
    weight_cached = jnp.where(valid_mask, jnp.exp(cached - row_top), 0.0)
    weight_fresh = jnp.where(causal, jnp.exp(fresh_scores - row_top), 0.0)
    row_total = (lax.optimization_barrier(jnp.sum(weight_cached, -1)) + lax.optimization_barrier(jnp.sum(weight_fresh, -1)))[..., None]
    probs_cached = (weight_cached / row_total).astype(jnp.bfloat16).astype(jnp.float32)
    probs_fresh = (weight_fresh / row_total).astype(jnp.bfloat16).astype(jnp.float32)
    heads_out = jnp.einsum('eskgc,ekcd->eskgd', probs_cached, value_cache.astype(jnp.float32))
    heads_out = heads_out + jnp.einsum('eskgt,etkd->eskgd', probs_fresh, values_now)
    return heads_out.reshape(env_count, step_count, feature_count)

def reference(residual, query_new, key_new, value_new, key_cache, value_cache, lengths, norm_gain, router, routes, w_gate, w_up, w_down):
    state = residual.astype(jnp.float32) + attend(query_new, key_new, value_new, key_cache, value_cache, lengths)
    attended = state.astype(jnp.bfloat16)
    squares = lax.optimization_barrier(jnp.sum(state * state, -1))
    root_mean = jnp.sqrt(squares / D + 1e-05)[..., None]
    scaled = state * norm_gain.astype(jnp.float32)
    logits = jnp.einsum('esd,dx->esx', scaled, router, precision=lax.Precision.HIGHEST) / root_mean
    normed = (scaled / root_mean).astype(jnp.bfloat16)
    expert_ids = jnp.arange(EXPERTS, dtype=jnp.int32)
    picked_logits = lax.optimization_barrier(jnp.sum(jnp.where(routes[..., None] == expert_ids, logits[:, :, None, :], 0.0), -1))
    first_gate = 1.0 / (1.0 + jnp.exp(picked_logits[..., 1] - picked_logits[..., 0]))
    second_gate = 1.0 - first_gate
    flat_rows = normed.reshape(ENVS * STEPS, D)

    def expert_rows(expert_id):
        gate_part = jnp.dot(flat_rows, w_gate[expert_id], preferred_element_type=jnp.float32)
        up_part = jnp.dot(flat_rows, w_up[expert_id], preferred_element_type=jnp.float32)
        hidden = (jax.nn.silu(gate_part) * up_part).astype(jnp.bfloat16)
        return jnp.dot(hidden, w_down[expert_id], preferred_element_type=jnp.float32).astype(jnp.bfloat16)
    outputs = lax.map(expert_rows, expert_ids)
    chosen = (routes.reshape(ENVS * STEPS, TOPK)[:, :, None] == expert_ids[None, None, :]).astype(jnp.float32)
    picked_rows = jnp.einsum('rkx,xrd->rkd', chosen, outputs.astype(jnp.float32), precision=lax.Precision.HIGHEST)
    picked_rows = picked_rows.reshape(ENVS, STEPS, TOPK, D)
    expert_mix = first_gate[..., None] * picked_rows[:, :, 0] + second_gate[..., None] * picked_rows[:, :, 1]
    return (attended, expert_mix.astype(jnp.bfloat16))
```

```python
import jax
import jax.numpy as jnp
from jax import lax
from jax.sharding import PartitionSpec as P

CAP = 16


def attend(query_new, key_new, value_new, key_cache, value_cache, lengths):
    env_count, step_count, feature_count = query_new.shape
    kv_count = key_cache.shape[1]
    context = key_cache.shape[2]
    head_dim = key_cache.shape[3]
    group_size = feature_count // (kv_count * head_dim)
    queries = query_new.reshape(env_count, step_count, kv_count, group_size, head_dim)
    keys_now = key_new.reshape(env_count, step_count, kv_count, head_dim)
    values_now = value_new.reshape(env_count, step_count, kv_count, head_dim)
    score_scale = head_dim ** (-0.5)
    cached = (
        jnp.einsum("eskgd,ekcd->eskgc", queries, key_cache, preferred_element_type=jnp.float32)
        * score_scale
    )
    fresh_scores = (
        jnp.einsum("eskgd,etkd->eskgt", queries, keys_now, preferred_element_type=jnp.float32)
        * score_scale
    )
    valid_mask = (lax.broadcasted_iota(jnp.int32, (env_count, context), 1) < lengths[:, None])[
        :, None, None, None, :
    ]
    causal = (
        lax.broadcasted_iota(jnp.int32, (step_count, step_count), 1)
        <= lax.broadcasted_iota(jnp.int32, (step_count, step_count), 0)
    )[None, :, None, None, :]
    cached = jnp.where(valid_mask, cached, -1e30)
    fresh_scores = jnp.where(causal, fresh_scores, -1e30)
    row_top = jnp.maximum(jnp.max(cached, -1), jnp.max(fresh_scores, -1))[..., None]
    weight_cached = jnp.where(valid_mask, jnp.exp(cached - row_top), 0.0)
    weight_fresh = jnp.where(causal, jnp.exp(fresh_scores - row_top), 0.0)
    row_total = (jnp.sum(weight_cached, -1) + jnp.sum(weight_fresh, -1))[..., None]
    probs_cached = (weight_cached / row_total).astype(jnp.bfloat16)
    probs_fresh = (weight_fresh / row_total).astype(jnp.bfloat16)
    heads_out = jnp.einsum(
        "eskgc,ekcd->eskgd", probs_cached, value_cache, preferred_element_type=jnp.float32
    )
    heads_out = heads_out + jnp.einsum(
        "eskgt,etkd->eskgd", probs_fresh, values_now, preferred_element_type=jnp.float32
    )
    return heads_out.reshape(env_count, step_count, feature_count)


def per_device(
    residual,
    query_new,
    key_new,
    value_new,
    key_cache,
    value_cache,
    lengths,
    norm_gain,
    router,
    routes,
    w_gate,
    w_up,
    w_down,
):
    env_count, step_count, slice_width = residual.shape
    local_experts, width, hidden_local = w_gate.shape
    experts = router.shape[1]
    topk = routes.shape[2]
    group_count = lax.axis_size("grp")
    tensor_count = lax.axis_size("tp")
    owner_count = lax.axis_size("ex")
    row_count = env_count * step_count
    state = residual.astype(jnp.float32) + attend(
        query_new, key_new, value_new, key_cache, value_cache, lengths
    )
    attended = state.astype(jnp.bfloat16)
    squares = jnp.sum(state * state, -1)
    scaled = state * norm_gain.astype(jnp.float32)
    partial_logits = jnp.einsum("esd,dx->esx", scaled, router, precision=lax.Precision.HIGHEST)
    squares, logits = lax.psum((squares, partial_logits), "tp")
    root_mean = jnp.sqrt(squares / width + 1e-05)[..., None]
    logits = logits / root_mean
    normed = (scaled / root_mean).astype(jnp.bfloat16)
    expert_ids = lax.broadcasted_iota(jnp.int32, (1, 1, 1, experts), 3)
    picked_logits = jnp.sum(
        jnp.where(routes[..., None] == expert_ids, logits[:, :, None, :], 0.0), -1
    )
    first_gate = 1.0 / (1.0 + jnp.exp(picked_logits[..., 1] - picked_logits[..., 0]))
    second_gate = 1.0 - first_gate
    flat_routes = routes.reshape(row_count * topk)
    expert_hits = (flat_routes[:, None] == lax.broadcasted_iota(jnp.int32, (1, experts), 1)).astype(
        jnp.int32
    )
    earlier = jnp.cumsum(expert_hits, axis=0) - expert_hits
    slot_ids = jnp.sum(earlier * expert_hits, axis=1)
    targets = flat_routes * CAP + slot_ids
    slot_table = lax.broadcasted_iota(jnp.int32, (1, experts * CAP), 1)
    placed = (
        (targets[:, None] == slot_table)
        .astype(jnp.bfloat16)
        .reshape(row_count, topk, experts * CAP)
    )
    sender = jnp.sum(placed, axis=1)
    packed = jnp.einsum(
        "rs,rd->sd",
        sender,
        normed.reshape(row_count, slice_width),
        preferred_element_type=jnp.float32,
    )
    outgoing = packed.astype(jnp.bfloat16).reshape(experts, CAP, slice_width)
    received = lax.all_to_all(outgoing, "ex", split_axis=0, concat_axis=0, tiled=True)
    received = received.reshape(1, owner_count, local_experts, CAP, slice_width)
    pieces = lax.all_gather(received, ("grp", "tp"), axis=0, tiled=True)

    pieces = pieces.reshape(
        group_count, tensor_count, owner_count, local_experts, CAP, slice_width
    )
    gate_split = w_gate.reshape(local_experts, tensor_count, slice_width, hidden_local)
    up_split = w_up.reshape(local_experts, tensor_count, slice_width, hidden_local)
    gate_sums = jnp.einsum(
        "gtajcd,jtdf->jgacf", pieces, gate_split, preferred_element_type=jnp.float32
    )
    up_sums = jnp.einsum("gtajcd,jtdf->jgacf", pieces, up_split, preferred_element_type=jnp.float32)
    hidden = (jax.nn.silu(gate_sums) * up_sums).astype(jnp.bfloat16)
    down_split = w_down.reshape(local_experts, hidden_local, tensor_count, slice_width)
    down_terms = jnp.einsum(
        "jgacf,jftd->gtajcd", hidden, down_split, preferred_element_type=jnp.float32
    )
    down_terms = down_terms.reshape(
        group_count * tensor_count, owner_count, local_experts, CAP, slice_width
    )
    summed = lax.psum_scatter(
        down_terms.astype(jnp.bfloat16), ("grp", "tp"), scatter_dimension=0, tiled=True
    ).astype(jnp.float32)
    returned = lax.all_to_all(
        summed[0].astype(jnp.bfloat16), "ex", split_axis=0, concat_axis=0, tiled=True
    )
    returned = returned.reshape(experts * CAP, slice_width)
    picked_rows = jnp.einsum("rks,sd->rkd", placed, returned, preferred_element_type=jnp.float32)
    picked_rows = picked_rows.reshape(env_count, step_count, topk, slice_width)
    expert_mix = (
        first_gate[..., None] * picked_rows[:, :, 0] + second_gate[..., None] * picked_rows[:, :, 1]
    )
    return (attended, expert_mix.astype(jnp.bfloat16))


def solution(mesh):
    return jax.shard_map(
        per_device,
        mesh=mesh,
        in_specs=(
            P(("grp", "ex"), None, "tp"),
            P(("grp", "ex"), None, "tp"),
            P(("grp", "ex"), None, "tp"),
            P(("grp", "ex"), None, "tp"),
            P(("grp", "ex"), "tp", None, None),
            P(("grp", "ex"), "tp", None, None),
            P(("grp", "ex")),
            P("tp"),
            P("tp", None),
            P(("grp", "ex"), None, None),
            P("ex", None, ("grp", "tp")),
            P("ex", None, ("grp", "tp")),
            P("ex", ("grp", "tp"), None),
        ),
        out_specs=(P(("grp", "ex"), None, "tp"), P(("grp", "ex"), None, "tp")),
        check_vma=False,
    )
```

```python
import jax
import jax.numpy as jnp
from jax import lax
from jax.sharding import PartitionSpec as P

CAP = 16


def attend(query_new, key_new, value_new, key_cache, value_cache, lengths):
    env_count, step_count, feature_count = query_new.shape
    kv_count = key_cache.shape[1]
    context = key_cache.shape[2]
    head_dim = key_cache.shape[3]
    group_size = feature_count // (kv_count * head_dim)
    queries = query_new.reshape(env_count, step_count, kv_count, group_size, head_dim)
    keys_now = key_new.reshape(env_count, step_count, kv_count, head_dim)
    values_now = value_new.reshape(env_count, step_count, kv_count, head_dim)
    score_scale = head_dim ** (-0.5)
    cached = (
        jnp.einsum("eskgd,ekcd->eskgc", queries, key_cache, preferred_element_type=jnp.float32)
        * score_scale
    )
    fresh_scores = (
        jnp.einsum("eskgd,etkd->eskgt", queries, keys_now, preferred_element_type=jnp.float32)
        * score_scale
    )
    valid_mask = (lax.broadcasted_iota(jnp.int32, (env_count, context), 1) < lengths[:, None])[
        :, None, None, None, :
    ]
    causal = (
        lax.broadcasted_iota(jnp.int32, (step_count, step_count), 1)
        <= lax.broadcasted_iota(jnp.int32, (step_count, step_count), 0)
    )[None, :, None, None, :]
    cached = jnp.where(valid_mask, cached, -1e30)
    fresh_scores = jnp.where(causal, fresh_scores, -1e30)
    row_top = jnp.maximum(jnp.max(cached, -1), jnp.max(fresh_scores, -1))[..., None]
    weight_cached = jnp.where(valid_mask, jnp.exp(cached - row_top), 0.0)
    weight_fresh = jnp.where(causal, jnp.exp(fresh_scores - row_top), 0.0)
    row_total = (jnp.sum(weight_cached, -1) + jnp.sum(weight_fresh, -1))[..., None]
    probs_cached = (weight_cached / row_total).astype(jnp.bfloat16)
    probs_fresh = (weight_fresh / row_total).astype(jnp.bfloat16)
    heads_out = jnp.einsum(
        "eskgc,ekcd->eskgd", probs_cached, value_cache, preferred_element_type=jnp.float32
    )
    heads_out = heads_out + jnp.einsum(
        "eskgt,etkd->eskgd", probs_fresh, values_now, preferred_element_type=jnp.float32
    )
    return heads_out.reshape(env_count, step_count, feature_count)


def ring_reduce_scatter(parts, axis, count, direction):
    me = lax.axis_index(axis)
    pairs = [(j, (j + direction) % count) for j in range(count)]

    def own(offset):
        chunk = (me - direction * offset) % count
        return lax.dynamic_index_in_dim(parts, chunk, 0, keepdims=False)

    total = own(1)
    for step in range(count - 1):
        arrived = lax.ppermute(total.astype(jnp.bfloat16), axis, pairs)
        total = arrived.astype(jnp.float32) + own(step + 2)
    return total


def per_device(
    residual,
    query_new,
    key_new,
    value_new,
    key_cache,
    value_cache,
    lengths,
    norm_gain,
    router,
    routes,
    w_gate,
    w_up,
    w_down,
):
    env_count, step_count, slice_width = residual.shape
    local_experts, width, hidden_local = w_gate.shape
    experts = router.shape[1]
    topk = routes.shape[2]
    group_count = lax.axis_size("grp")
    tensor_count = lax.axis_size("tp")
    owner_count = lax.axis_size("ex")
    row_count = env_count * step_count
    state = residual.astype(jnp.float32) + attend(
        query_new, key_new, value_new, key_cache, value_cache, lengths
    )
    attended = state.astype(jnp.bfloat16)
    squares = jnp.sum(state * state, -1)
    scaled = state * norm_gain.astype(jnp.float32)
    partial_logits = jnp.einsum("esd,dx->esx", scaled, router, precision=lax.Precision.HIGHEST)
    squares, logits = lax.psum((squares, partial_logits), "tp")
    root_mean = jnp.sqrt(squares / width + 1e-05)[..., None]
    logits = logits / root_mean
    normed = (scaled / root_mean).astype(jnp.bfloat16)
    expert_ids = lax.broadcasted_iota(jnp.int32, (1, 1, 1, experts), 3)
    picked_logits = jnp.sum(
        jnp.where(routes[..., None] == expert_ids, logits[:, :, None, :], 0.0), -1
    )
    first_gate = 1.0 / (1.0 + jnp.exp(picked_logits[..., 1] - picked_logits[..., 0]))
    second_gate = 1.0 - first_gate
    flat_routes = routes.reshape(row_count * topk)
    expert_hits = (flat_routes[:, None] == lax.broadcasted_iota(jnp.int32, (1, experts), 1)).astype(
        jnp.int32
    )
    earlier = jnp.cumsum(expert_hits, axis=0) - expert_hits
    slot_ids = jnp.sum(earlier * expert_hits, axis=1)
    targets = flat_routes * CAP + slot_ids
    slot_table = lax.broadcasted_iota(jnp.int32, (1, experts * CAP), 1)
    placed = (
        (targets[:, None] == slot_table)
        .astype(jnp.bfloat16)
        .reshape(row_count, topk, experts * CAP)
    )
    sender = jnp.sum(placed, axis=1)
    packed = jnp.einsum(
        "rs,rd->sd",
        sender,
        normed.reshape(row_count, slice_width),
        preferred_element_type=jnp.float32,
    )
    outgoing = packed.astype(jnp.bfloat16).reshape(experts, CAP, slice_width)
    received = lax.all_to_all(outgoing, "ex", split_axis=0, concat_axis=0, tiled=True)
    received = received.reshape(1, owner_count, local_experts, CAP, slice_width)
    pieces = lax.all_gather(received, ("grp", "tp"), axis=0, tiled=True)

    pieces = pieces.reshape(
        group_count, tensor_count, owner_count, local_experts, CAP, slice_width
    )
    gate_split = w_gate.reshape(local_experts, tensor_count, slice_width, hidden_local)
    up_split = w_up.reshape(local_experts, tensor_count, slice_width, hidden_local)
    gate_sums = jnp.einsum(
        "gtajcd,jtdf->jgacf", pieces, gate_split, preferred_element_type=jnp.float32
    )
    up_sums = jnp.einsum("gtajcd,jtdf->jgacf", pieces, up_split, preferred_element_type=jnp.float32)
    hidden = (jax.nn.silu(gate_sums) * up_sums).astype(jnp.bfloat16)
    down_split = w_down.reshape(local_experts, hidden_local, tensor_count, slice_width)
    down_terms = jnp.einsum(
        "jgacf,jftd->tgajcd", hidden, down_split, preferred_element_type=jnp.float32
    )
    half = group_count // 2
    clockwise = ring_reduce_scatter(down_terms[:, :half], "tp", tensor_count, 1)
    counter = ring_reduce_scatter(down_terms[:, half:], "tp", tensor_count, -1)
    over_tp = jnp.concatenate([clockwise, counter], axis=0).astype(jnp.bfloat16)
    summed = lax.psum_scatter(over_tp, "grp", scatter_dimension=0, tiled=True)
    summed = summed.astype(jnp.float32)
    returned = lax.all_to_all(
        summed[0].astype(jnp.bfloat16), "ex", split_axis=0, concat_axis=0, tiled=True
    )
    returned = returned.reshape(experts * CAP, slice_width)
    picked_rows = jnp.einsum("rks,sd->rkd", placed, returned, preferred_element_type=jnp.float32)
    picked_rows = picked_rows.reshape(env_count, step_count, topk, slice_width)
    expert_mix = (
        first_gate[..., None] * picked_rows[:, :, 0] + second_gate[..., None] * picked_rows[:, :, 1]
    )
    return (attended, expert_mix.astype(jnp.bfloat16))


def solution(mesh):
    return jax.shard_map(
        per_device,
        mesh=mesh,
        in_specs=(
            P(("grp", "ex"), None, "tp"),
            P(("grp", "ex"), None, "tp"),
            P(("grp", "ex"), None, "tp"),
            P(("grp", "ex"), None, "tp"),
            P(("grp", "ex"), "tp", None, None),
            P(("grp", "ex"), "tp", None, None),
            P(("grp", "ex")),
            P("tp"),
            P("tp", None),
            P(("grp", "ex"), None, None),
            P("ex", None, ("grp", "tp")),
            P("ex", None, ("grp", "tp")),
            P("ex", ("grp", "tp"), None),
        ),
        out_specs=(P(("grp", "ex"), None, "tp"), P(("grp", "ex"), None, "tp")),
        check_vma=False,
    )
```

```python
import jax
import jax.numpy as jnp
from jax import lax
from jax.sharding import PartitionSpec as P

CAP = 16


def attend(query_new, key_new, value_new, key_cache, value_cache, lengths):
    env_count, step_count, feature_count = query_new.shape
    kv_count = key_cache.shape[1]
    context = key_cache.shape[2]
    head_dim = key_cache.shape[3]
    group_size = feature_count // (kv_count * head_dim)
    queries = query_new.reshape(env_count, step_count, kv_count, group_size, head_dim)
    keys_now = key_new.reshape(env_count, step_count, kv_count, head_dim)
    values_now = value_new.reshape(env_count, step_count, kv_count, head_dim)
    score_scale = head_dim ** (-0.5)
    cached = (
        jnp.einsum("eskgd,ekcd->eskgc", queries, key_cache, preferred_element_type=jnp.float32)
        * score_scale
    )
    fresh_scores = (
        jnp.einsum("eskgd,etkd->eskgt", queries, keys_now, preferred_element_type=jnp.float32)
        * score_scale
    )
    valid_mask = (lax.broadcasted_iota(jnp.int32, (env_count, context), 1) < lengths[:, None])[
        :, None, None, None, :
    ]
    causal = (
        lax.broadcasted_iota(jnp.int32, (step_count, step_count), 1)
        <= lax.broadcasted_iota(jnp.int32, (step_count, step_count), 0)
    )[None, :, None, None, :]
    cached = jnp.where(valid_mask, cached, -1e30)
    fresh_scores = jnp.where(causal, fresh_scores, -1e30)
    row_top = jnp.maximum(jnp.max(cached, -1), jnp.max(fresh_scores, -1))[..., None]
    weight_cached = jnp.where(valid_mask, jnp.exp(cached - row_top), 0.0)
    weight_fresh = jnp.where(causal, jnp.exp(fresh_scores - row_top), 0.0)
    row_total = (jnp.sum(weight_cached, -1) + jnp.sum(weight_fresh, -1))[..., None]
    probs_cached = (weight_cached / row_total).astype(jnp.bfloat16)
    probs_fresh = (weight_fresh / row_total).astype(jnp.bfloat16)
    heads_out = jnp.einsum(
        "eskgc,ekcd->eskgd", probs_cached, value_cache, preferred_element_type=jnp.float32
    )
    heads_out = heads_out + jnp.einsum(
        "eskgt,etkd->eskgd", probs_fresh, values_now, preferred_element_type=jnp.float32
    )
    return heads_out.reshape(env_count, step_count, feature_count)


def ring_reduce_scatter(parts, axis, count, direction):
    me = lax.axis_index(axis)
    pairs = [(j, (j + direction) % count) for j in range(count)]

    def own(offset):
        chunk = (me - direction * offset) % count
        return lax.dynamic_index_in_dim(parts, chunk, 0, keepdims=False)

    total = own(1)
    for step in range(count - 1):
        arrived = lax.ppermute(total.astype(jnp.bfloat16), axis, pairs)
        total = arrived.astype(jnp.float32) + own(step + 2)
    return total


def both_ways(forward, backward, axis, joined):
    count = lax.axis_size(axis)
    return jnp.concatenate(
        [
            ring_reduce_scatter(forward, axis, count, 1),
            ring_reduce_scatter(backward, axis, count, -1),
        ],
        axis=joined,
    )


def per_device(
    residual,
    query_new,
    key_new,
    value_new,
    key_cache,
    value_cache,
    lengths,
    norm_gain,
    router,
    routes,
    w_gate,
    w_up,
    w_down,
):
    env_count, step_count, slice_width = residual.shape
    local_experts, width, hidden_local = w_gate.shape
    experts = router.shape[1]
    topk = routes.shape[2]
    group_count = lax.axis_size("grp")
    tensor_count = lax.axis_size("tp")
    owner_count = lax.axis_size("ex")
    row_count = env_count * step_count
    state = residual.astype(jnp.float32) + attend(
        query_new, key_new, value_new, key_cache, value_cache, lengths
    )
    attended = state.astype(jnp.bfloat16)
    squares = jnp.sum(state * state, -1)
    scaled = state * norm_gain.astype(jnp.float32)
    partial_logits = jnp.einsum("esd,dx->esx", scaled, router, precision=lax.Precision.HIGHEST)
    squares, logits = lax.psum((squares, partial_logits), "tp")
    root_mean = jnp.sqrt(squares / width + 1e-05)[..., None]
    logits = logits / root_mean
    normed = (scaled / root_mean).astype(jnp.bfloat16)
    expert_ids = lax.broadcasted_iota(jnp.int32, (1, 1, 1, experts), 3)
    picked_logits = jnp.sum(
        jnp.where(routes[..., None] == expert_ids, logits[:, :, None, :], 0.0), -1
    )
    first_gate = 1.0 / (1.0 + jnp.exp(picked_logits[..., 1] - picked_logits[..., 0]))
    second_gate = 1.0 - first_gate
    flat_routes = routes.reshape(row_count * topk)
    expert_hits = (flat_routes[:, None] == lax.broadcasted_iota(jnp.int32, (1, experts), 1)).astype(
        jnp.int32
    )
    earlier = jnp.cumsum(expert_hits, axis=0) - expert_hits
    slot_ids = jnp.sum(earlier * expert_hits, axis=1)
    targets = flat_routes * CAP + slot_ids
    slot_table = lax.broadcasted_iota(jnp.int32, (1, experts * CAP), 1)
    placed = (
        (targets[:, None] == slot_table)
        .astype(jnp.bfloat16)
        .reshape(row_count, topk, experts * CAP)
    )
    sender = jnp.sum(placed, axis=1)
    packed = jnp.einsum(
        "rs,rd->sd",
        sender,
        normed.reshape(row_count, slice_width),
        preferred_element_type=jnp.float32,
    )
    outgoing = packed.astype(jnp.bfloat16).reshape(experts, CAP, slice_width)
    received = lax.all_to_all(outgoing, "ex", split_axis=0, concat_axis=0, tiled=True)
    received = received.reshape(1, owner_count, local_experts, CAP, slice_width)
    pieces = lax.all_gather(received, ("grp", "tp"), axis=0, tiled=True)

    pieces = pieces.reshape(
        group_count, tensor_count, owner_count, local_experts, CAP, slice_width
    )
    gate_split = w_gate.reshape(local_experts, tensor_count, slice_width, hidden_local)
    up_split = w_up.reshape(local_experts, tensor_count, slice_width, hidden_local)
    gate_sums = jnp.einsum(
        "gtajcd,jtdf->jgacf", pieces, gate_split, preferred_element_type=jnp.float32
    )
    up_sums = jnp.einsum("gtajcd,jtdf->jgacf", pieces, up_split, preferred_element_type=jnp.float32)
    hidden = (jax.nn.silu(gate_sums) * up_sums).astype(jnp.bfloat16)
    down_split = w_down.reshape(local_experts, hidden_local, tensor_count, slice_width)
    owner_half = owner_count // 2
    group_half = group_count // 2
    tensor_half = tensor_count // 2
    slot_half = CAP // 2

    def down(rows, columns, spec):
        return jnp.einsum(spec, rows, columns, preferred_element_type=jnp.float32)

    z_rows = hidden[:, :, :owner_half]
    y_rows = hidden[:, :, owner_half:]
    z_first = both_ways(
        down(z_rows[:, :group_half], down_split, "jgacf,jftd->tgajcd"),
        down(z_rows[:, group_half:], down_split, "jgacf,jftd->tgajcd"),
        "tp",
        0,
    )
    y_first = both_ways(
        down(y_rows, down_split[:, :, :tensor_half], "jgacf,jftd->gtajcd"),
        down(y_rows, down_split[:, :, tensor_half:], "jgacf,jftd->gtajcd"),
        "grp",
        0,
    )
    z_done = both_ways(z_first[:, :, :, :slot_half], z_first[:, :, :, slot_half:], "grp", 2)
    y_done = both_ways(y_first[:, :, :, :slot_half], y_first[:, :, :, slot_half:], "tp", 2)
    summed = jnp.concatenate([z_done, y_done], axis=0)
    returned = lax.all_to_all(
        summed.astype(jnp.bfloat16), "ex", split_axis=0, concat_axis=0, tiled=True
    )
    returned = returned.reshape(experts * CAP, slice_width)
    picked_rows = jnp.einsum("rks,sd->rkd", placed, returned, preferred_element_type=jnp.float32)
    picked_rows = picked_rows.reshape(env_count, step_count, topk, slice_width)
    expert_mix = (
        first_gate[..., None] * picked_rows[:, :, 0] + second_gate[..., None] * picked_rows[:, :, 1]
    )
    return (attended, expert_mix.astype(jnp.bfloat16))


def solution(mesh):
    return jax.shard_map(
        per_device,
        mesh=mesh,
        in_specs=(
            P(("grp", "ex"), None, "tp"),
            P(("grp", "ex"), None, "tp"),
            P(("grp", "ex"), None, "tp"),
            P(("grp", "ex"), None, "tp"),
            P(("grp", "ex"), "tp", None, None),
            P(("grp", "ex"), "tp", None, None),
            P(("grp", "ex")),
            P("tp"),
            P("tp", None),
            P(("grp", "ex"), None, None),
            P("ex", None, ("grp", "tp")),
            P("ex", None, ("grp", "tp")),
            P("ex", ("grp", "tp"), None),
        ),
        out_specs=(P(("grp", "ex"), None, "tp"), P(("grp", "ex"), None, "tp")),
        check_vma=False,
    )
```

```python
import jax
import jax.numpy as jnp
from jax import lax
from jax.sharding import PartitionSpec as P

CAP = 16


def attend(query_new, key_new, value_new, key_cache, value_cache, lengths):
    env_count, step_count, feature_count = query_new.shape
    kv_count = key_cache.shape[1]
    context = key_cache.shape[2]
    head_dim = key_cache.shape[3]
    group_size = feature_count // (kv_count * head_dim)
    queries = query_new.reshape(env_count, step_count, kv_count, group_size, head_dim)
    keys_now = key_new.reshape(env_count, step_count, kv_count, head_dim)
    values_now = value_new.reshape(env_count, step_count, kv_count, head_dim)
    score_scale = head_dim ** (-0.5)
    cached = (
        jnp.einsum("eskgd,ekcd->eskgc", queries, key_cache, preferred_element_type=jnp.float32)
        * score_scale
    )
    fresh_scores = (
        jnp.einsum("eskgd,etkd->eskgt", queries, keys_now, preferred_element_type=jnp.float32)
        * score_scale
    )
    valid_mask = (lax.broadcasted_iota(jnp.int32, (env_count, context), 1) < lengths[:, None])[
        :, None, None, None, :
    ]
    causal = (
        lax.broadcasted_iota(jnp.int32, (step_count, step_count), 1)
        <= lax.broadcasted_iota(jnp.int32, (step_count, step_count), 0)
    )[None, :, None, None, :]
    cached = jnp.where(valid_mask, cached, -1e30)
    fresh_scores = jnp.where(causal, fresh_scores, -1e30)
    row_top = jnp.maximum(jnp.max(cached, -1), jnp.max(fresh_scores, -1))[..., None]
    weight_cached = jnp.where(valid_mask, jnp.exp(cached - row_top), 0.0)
    weight_fresh = jnp.where(causal, jnp.exp(fresh_scores - row_top), 0.0)
    row_total = (jnp.sum(weight_cached, -1) + jnp.sum(weight_fresh, -1))[..., None]
    probs_cached = (weight_cached / row_total).astype(jnp.bfloat16)
    probs_fresh = (weight_fresh / row_total).astype(jnp.bfloat16)
    heads_out = jnp.einsum(
        "eskgc,ekcd->eskgd", probs_cached, value_cache, preferred_element_type=jnp.float32
    )
    heads_out = heads_out + jnp.einsum(
        "eskgt,etkd->eskgd", probs_fresh, values_now, preferred_element_type=jnp.float32
    )
    return heads_out.reshape(env_count, step_count, feature_count)


def ring_reduce_scatter(parts, axis, count, direction):
    me = lax.axis_index(axis)
    pairs = [(j, (j + direction) % count) for j in range(count)]

    def own(offset):
        chunk = (me - direction * offset) % count
        return lax.dynamic_index_in_dim(parts, chunk, 0, keepdims=False)

    total = own(1)
    for step in range(count - 1):
        arrived = lax.ppermute(total.astype(jnp.bfloat16), axis, pairs)
        total = arrived.astype(jnp.float32) + own(step + 2)
    return total


def both_ways(forward, backward, axis, joined):
    count = lax.axis_size(axis)
    return jnp.concatenate(
        [
            ring_reduce_scatter(forward, axis, count, 1),
            ring_reduce_scatter(backward, axis, count, -1),
        ],
        axis=joined,
    )


def exchange_sum(parts, axis):
    moved = lax.all_to_all(parts.astype(jnp.bfloat16), axis, 0, 0, tiled=True)
    return jnp.sum(moved.astype(jnp.float32), axis=0)


def per_device(
    residual,
    query_new,
    key_new,
    value_new,
    key_cache,
    value_cache,
    lengths,
    norm_gain,
    router,
    routes,
    w_gate,
    w_up,
    w_down,
):
    env_count, step_count, slice_width = residual.shape
    local_experts, width, hidden_local = w_gate.shape
    experts = router.shape[1]
    topk = routes.shape[2]
    group_count = lax.axis_size("grp")
    tensor_count = lax.axis_size("tp")
    owner_count = lax.axis_size("ex")
    row_count = env_count * step_count
    state = residual.astype(jnp.float32) + attend(
        query_new, key_new, value_new, key_cache, value_cache, lengths
    )
    attended = state.astype(jnp.bfloat16)
    squares = jnp.sum(state * state, -1)
    scaled = state * norm_gain.astype(jnp.float32)
    partial_logits = jnp.einsum("esd,dx->esx", scaled, router, precision=lax.Precision.HIGHEST)
    squares, logits = lax.psum((squares, partial_logits), "tp")
    root_mean = jnp.sqrt(squares / width + 1e-05)[..., None]
    logits = logits / root_mean
    normed = (scaled / root_mean).astype(jnp.bfloat16)
    expert_ids = lax.broadcasted_iota(jnp.int32, (1, 1, 1, experts), 3)
    picked_logits = jnp.sum(
        jnp.where(routes[..., None] == expert_ids, logits[:, :, None, :], 0.0), -1
    )
    first_gate = 1.0 / (1.0 + jnp.exp(picked_logits[..., 1] - picked_logits[..., 0]))
    second_gate = 1.0 - first_gate
    flat_routes = routes.reshape(row_count * topk)
    expert_hits = (flat_routes[:, None] == lax.broadcasted_iota(jnp.int32, (1, experts), 1)).astype(
        jnp.int32
    )
    earlier = jnp.cumsum(expert_hits, axis=0) - expert_hits
    slot_ids = jnp.sum(earlier * expert_hits, axis=1)
    targets = flat_routes * CAP + slot_ids
    slot_table = lax.broadcasted_iota(jnp.int32, (1, experts * CAP), 1)
    placed = (
        (targets[:, None] == slot_table)
        .astype(jnp.bfloat16)
        .reshape(row_count, topk, experts * CAP)
    )
    sender = jnp.sum(placed, axis=1)
    packed = jnp.einsum(
        "rs,rd->sd",
        sender,
        normed.reshape(row_count, slice_width),
        preferred_element_type=jnp.float32,
    )
    outgoing = packed.astype(jnp.bfloat16).reshape(experts, CAP, slice_width)
    received = lax.all_to_all(outgoing, "ex", split_axis=0, concat_axis=0, tiled=True)
    received = received.reshape(1, owner_count, local_experts, CAP, slice_width)
    pieces = lax.all_gather(received, ("grp", "tp"), axis=0, tiled=True)

    pieces = pieces.reshape(
        group_count, tensor_count, owner_count, local_experts, CAP, slice_width
    )
    gate_split = w_gate.reshape(local_experts, tensor_count, slice_width, hidden_local)
    up_split = w_up.reshape(local_experts, tensor_count, slice_width, hidden_local)
    gate_sums = jnp.einsum(
        "gtajcd,jtdf->jgacf", pieces, gate_split, preferred_element_type=jnp.float32
    )
    up_sums = jnp.einsum("gtajcd,jtdf->jgacf", pieces, up_split, preferred_element_type=jnp.float32)
    hidden = (jax.nn.silu(gate_sums) * up_sums).astype(jnp.bfloat16)
    down_split = w_down.reshape(local_experts, hidden_local, tensor_count, slice_width)
    owner_half = owner_count // 2
    group_half = group_count // 2
    tensor_half = tensor_count // 2

    def down(rows, columns, spec):
        return jnp.einsum(spec, rows, columns, preferred_element_type=jnp.float32)

    z_rows = hidden[:, :, :owner_half]
    y_rows = hidden[:, :, owner_half:]
    z_first = both_ways(
        down(z_rows[:, :group_half], down_split, "jgacf,jftd->tgajcd"),
        down(z_rows[:, group_half:], down_split, "jgacf,jftd->tgajcd"),
        "tp",
        0,
    )
    y_first = both_ways(
        down(y_rows, down_split[:, :, :tensor_half], "jgacf,jftd->gtajcd"),
        down(y_rows, down_split[:, :, tensor_half:], "jgacf,jftd->gtajcd"),
        "grp",
        0,
    )
    z_done = exchange_sum(z_first, "grp")
    y_done = exchange_sum(y_first, "tp")
    summed = jnp.concatenate([z_done, y_done], axis=0)
    returned = lax.all_to_all(
        summed.astype(jnp.bfloat16), "ex", split_axis=0, concat_axis=0, tiled=True
    )
    returned = returned.reshape(experts * CAP, slice_width)
    picked_rows = jnp.einsum("rks,sd->rkd", placed, returned, preferred_element_type=jnp.float32)
    picked_rows = picked_rows.reshape(env_count, step_count, topk, slice_width)
    expert_mix = (
        first_gate[..., None] * picked_rows[:, :, 0] + second_gate[..., None] * picked_rows[:, :, 1]
    )
    return (attended, expert_mix.astype(jnp.bfloat16))


def solution(mesh):
    return jax.shard_map(
        per_device,
        mesh=mesh,
        in_specs=(
            P(("grp", "ex"), None, "tp"),
            P(("grp", "ex"), None, "tp"),
            P(("grp", "ex"), None, "tp"),
            P(("grp", "ex"), None, "tp"),
            P(("grp", "ex"), "tp", None, None),
            P(("grp", "ex"), "tp", None, None),
            P(("grp", "ex")),
            P("tp"),
            P("tp", None),
            P(("grp", "ex"), None, None),
            P("ex", None, ("grp", "tp")),
            P("ex", None, ("grp", "tp")),
            P("ex", ("grp", "tp"), None),
        ),
        out_specs=(P(("grp", "ex"), None, "tp"), P(("grp", "ex"), None, "tp")),
        check_vma=False,
    )
```

```python
import jax
import jax.numpy as jnp
from jax import lax
from jax.sharding import PartitionSpec as P

CAP = 16


def attend(query_new, key_new, value_new, key_cache, value_cache, lengths):
    env_count, step_count, feature_count = query_new.shape
    kv_count = key_cache.shape[1]
    context = key_cache.shape[2]
    head_dim = key_cache.shape[3]
    group_size = feature_count // (kv_count * head_dim)
    queries = query_new.reshape(env_count, step_count, kv_count, group_size, head_dim)
    keys_now = key_new.reshape(env_count, step_count, kv_count, head_dim)
    values_now = value_new.reshape(env_count, step_count, kv_count, head_dim)
    score_scale = head_dim ** (-0.5)
    cached = (
        jnp.einsum("eskgd,ekcd->eskgc", queries, key_cache, preferred_element_type=jnp.float32)
        * score_scale
    )
    fresh_scores = (
        jnp.einsum("eskgd,etkd->eskgt", queries, keys_now, preferred_element_type=jnp.float32)
        * score_scale
    )
    valid_mask = (lax.broadcasted_iota(jnp.int32, (env_count, context), 1) < lengths[:, None])[
        :, None, None, None, :
    ]
    causal = (
        lax.broadcasted_iota(jnp.int32, (step_count, step_count), 1)
        <= lax.broadcasted_iota(jnp.int32, (step_count, step_count), 0)
    )[None, :, None, None, :]
    cached = jnp.where(valid_mask, cached, -1e30)
    fresh_scores = jnp.where(causal, fresh_scores, -1e30)
    row_top = jnp.maximum(jnp.max(cached, -1), jnp.max(fresh_scores, -1))[..., None]
    weight_cached = jnp.where(valid_mask, jnp.exp(cached - row_top), 0.0)
    weight_fresh = jnp.where(causal, jnp.exp(fresh_scores - row_top), 0.0)
    row_total = (jnp.sum(weight_cached, -1) + jnp.sum(weight_fresh, -1))[..., None]
    probs_cached = (weight_cached / row_total).astype(jnp.bfloat16)
    probs_fresh = (weight_fresh / row_total).astype(jnp.bfloat16)
    heads_out = jnp.einsum(
        "eskgc,ekcd->eskgd", probs_cached, value_cache, preferred_element_type=jnp.float32
    )
    heads_out = heads_out + jnp.einsum(
        "eskgt,etkd->eskgd", probs_fresh, values_now, preferred_element_type=jnp.float32
    )
    return heads_out.reshape(env_count, step_count, feature_count)


def ring_reduce_scatter(parts, axis, count, direction):
    me = lax.axis_index(axis)
    pairs = [(j, (j + direction) % count) for j in range(count)]

    def own(offset):
        chunk = (me - direction * offset) % count
        return lax.dynamic_index_in_dim(parts, chunk, 0, keepdims=False)

    total = own(1)
    for step in range(count - 1):
        arrived = lax.ppermute(total.astype(jnp.bfloat16), axis, pairs)
        total = arrived.astype(jnp.float32) + own(step + 2)
    return total


def both_ways(forward, backward, axis, joined):
    count = lax.axis_size(axis)
    return jnp.concatenate(
        [
            ring_reduce_scatter(forward, axis, count, 1),
            ring_reduce_scatter(backward, axis, count, -1),
        ],
        axis=joined,
    )


def exchange_sum(parts, axis):
    moved = lax.all_to_all(parts.astype(jnp.bfloat16), axis, 0, 0, tiled=True)
    return jnp.sum(moved.astype(jnp.float32), axis=0)


def per_device(
    residual,
    query_new,
    key_new,
    value_new,
    key_cache,
    value_cache,
    lengths,
    norm_gain,
    router,
    routes,
    w_gate,
    w_up,
    w_down,
):
    env_count, step_count, slice_width = residual.shape
    local_experts, width, hidden_local = w_gate.shape
    experts = router.shape[1]
    topk = routes.shape[2]
    group_count = lax.axis_size("grp")
    tensor_count = lax.axis_size("tp")
    owner_count = lax.axis_size("ex")
    row_count = env_count * step_count
    state = residual.astype(jnp.float32) + attend(
        query_new, key_new, value_new, key_cache, value_cache, lengths
    )
    attended = state.astype(jnp.bfloat16)
    squares = jnp.sum(state * state, -1)
    scaled = state * norm_gain.astype(jnp.float32)
    partial_logits = jnp.einsum("esd,dx->esx", scaled, router, precision=lax.Precision.HIGHEST)
    squares, logits = lax.psum((squares, partial_logits), "tp")
    root_mean = jnp.sqrt(squares / width + 1e-05)[..., None]
    logits = logits / root_mean
    normed = (scaled / root_mean).astype(jnp.bfloat16)
    expert_ids = lax.broadcasted_iota(jnp.int32, (1, 1, 1, experts), 3)
    picked_logits = jnp.sum(
        jnp.where(routes[..., None] == expert_ids, logits[:, :, None, :], 0.0), -1
    )
    first_gate = 1.0 / (1.0 + jnp.exp(picked_logits[..., 1] - picked_logits[..., 0]))
    second_gate = 1.0 - first_gate
    flat_routes = routes.reshape(row_count * topk)
    expert_hits = (flat_routes[:, None] == lax.broadcasted_iota(jnp.int32, (1, experts), 1)).astype(
        jnp.int32
    )
    earlier = jnp.cumsum(expert_hits, axis=0) - expert_hits
    slot_ids = jnp.sum(earlier * expert_hits, axis=1)
    targets = flat_routes * CAP + slot_ids
    slot_table = lax.broadcasted_iota(jnp.int32, (1, experts * CAP), 1)
    placed = (
        (targets[:, None] == slot_table)
        .astype(jnp.bfloat16)
        .reshape(row_count, topk, experts * CAP)
    )
    sender = jnp.sum(placed, axis=1)
    packed = jnp.einsum(
        "rs,rd->sd",
        sender,
        normed.reshape(row_count, slice_width),
        preferred_element_type=jnp.float32,
    )
    outgoing = packed.astype(jnp.bfloat16).reshape(experts, CAP, slice_width)
    received = lax.all_to_all(outgoing, "ex", split_axis=0, concat_axis=0, tiled=True)
    received = received.reshape(1, owner_count, local_experts, CAP, slice_width)
    pieces = lax.all_gather(received, ("grp", "tp"), axis=0, tiled=True)

    pieces = pieces.reshape(
        group_count, tensor_count, owner_count, local_experts, CAP, slice_width
    )
    gate_split = w_gate.reshape(local_experts, tensor_count, slice_width, hidden_local)
    up_split = w_up.reshape(local_experts, tensor_count, slice_width, hidden_local)
    gate_sums = jnp.einsum(
        "gtajcd,jtdf->jgacf", pieces, gate_split, preferred_element_type=jnp.float32
    )
    up_sums = jnp.einsum("gtajcd,jtdf->jgacf", pieces, up_split, preferred_element_type=jnp.float32)
    hidden = (jax.nn.silu(gate_sums) * up_sums).astype(jnp.bfloat16)
    down_split = w_down.reshape(local_experts, hidden_local, tensor_count, slice_width)
    owner_half = owner_count // 2
    group_half = group_count // 2

    def down(rows, columns, spec):
        return jnp.einsum(spec, rows, columns, preferred_element_type=jnp.float32)

    z_rows = hidden[:, :, :owner_half]
    y_rows = hidden[:, :, owner_half:]
    z_first = both_ways(
        down(z_rows[:, :group_half], down_split, "jgacf,jftd->tgajcd"),
        down(z_rows[:, group_half:], down_split, "jgacf,jftd->tgajcd"),
        "tp",
        0,
    )
    y_first = exchange_sum(down(y_rows, down_split, "jgacf,jftd->gtajcd"), "grp")
    z_done = exchange_sum(z_first, "grp")
    y_done = exchange_sum(y_first, "tp")
    summed = jnp.concatenate([z_done, y_done], axis=0)
    returned = lax.all_to_all(
        summed.astype(jnp.bfloat16), "ex", split_axis=0, concat_axis=0, tiled=True
    )
    returned = returned.reshape(experts * CAP, slice_width)
    picked_rows = jnp.einsum("rks,sd->rkd", placed, returned, preferred_element_type=jnp.float32)
    picked_rows = picked_rows.reshape(env_count, step_count, topk, slice_width)
    expert_mix = (
        first_gate[..., None] * picked_rows[:, :, 0] + second_gate[..., None] * picked_rows[:, :, 1]
    )
    return (attended, expert_mix.astype(jnp.bfloat16))


def solution(mesh):
    return jax.shard_map(
        per_device,
        mesh=mesh,
        in_specs=(
            P(("grp", "ex"), None, "tp"),
            P(("grp", "ex"), None, "tp"),
            P(("grp", "ex"), None, "tp"),
            P(("grp", "ex"), None, "tp"),
            P(("grp", "ex"), "tp", None, None),
            P(("grp", "ex"), "tp", None, None),
            P(("grp", "ex")),
            P("tp"),
            P("tp", None),
            P(("grp", "ex"), None, None),
            P("ex", None, ("grp", "tp")),
            P("ex", None, ("grp", "tp")),
            P("ex", ("grp", "tp"), None),
        ),
        out_specs=(P(("grp", "ex"), None, "tp"), P(("grp", "ex"), None, "tp")),
        check_vma=False,
    )
```

```python
import jax
import jax.numpy as jnp
from jax import lax
from jax.sharding import PartitionSpec as P

CAP = 16


def attend(query_new, key_new, value_new, key_cache, value_cache, lengths):
    env_count, step_count, feature_count = query_new.shape
    kv_count = key_cache.shape[1]
    context = key_cache.shape[2]
    head_dim = key_cache.shape[3]
    group_size = feature_count // (kv_count * head_dim)
    queries = query_new.reshape(env_count, step_count, kv_count, group_size, head_dim)
    keys_now = key_new.reshape(env_count, step_count, kv_count, head_dim)
    values_now = value_new.reshape(env_count, step_count, kv_count, head_dim)
    score_scale = head_dim ** (-0.5)
    cached = (
        jnp.einsum("eskgd,ekcd->eskgc", queries, key_cache, preferred_element_type=jnp.float32)
        * score_scale
    )
    fresh_scores = (
        jnp.einsum("eskgd,etkd->eskgt", queries, keys_now, preferred_element_type=jnp.float32)
        * score_scale
    )
    valid_mask = (lax.broadcasted_iota(jnp.int32, (env_count, context), 1) < lengths[:, None])[
        :, None, None, None, :
    ]
    causal = (
        lax.broadcasted_iota(jnp.int32, (step_count, step_count), 1)
        <= lax.broadcasted_iota(jnp.int32, (step_count, step_count), 0)
    )[None, :, None, None, :]
    cached = jnp.where(valid_mask, cached, -1e30)
    fresh_scores = jnp.where(causal, fresh_scores, -1e30)
    row_top = jnp.maximum(jnp.max(cached, -1), jnp.max(fresh_scores, -1))[..., None]
    weight_cached = jnp.where(valid_mask, jnp.exp(cached - row_top), 0.0)
    weight_fresh = jnp.where(causal, jnp.exp(fresh_scores - row_top), 0.0)
    row_total = (jnp.sum(weight_cached, -1) + jnp.sum(weight_fresh, -1))[..., None]
    probs_cached = (weight_cached / row_total).astype(jnp.bfloat16)
    probs_fresh = (weight_fresh / row_total).astype(jnp.bfloat16)
    heads_out = jnp.einsum(
        "eskgc,ekcd->eskgd", probs_cached, value_cache, preferred_element_type=jnp.float32
    )
    heads_out = heads_out + jnp.einsum(
        "eskgt,etkd->eskgd", probs_fresh, values_now, preferred_element_type=jnp.float32
    )
    return heads_out.reshape(env_count, step_count, feature_count)


def ring_reduce_scatter(parts, axis, count, direction):
    me = lax.axis_index(axis)
    pairs = [(j, (j + direction) % count) for j in range(count)]

    def own(offset):
        chunk = (me - direction * offset) % count
        return lax.dynamic_index_in_dim(parts, chunk, 0, keepdims=False)

    total = own(1)
    for step in range(count - 1):
        arrived = lax.ppermute(total.astype(jnp.bfloat16), axis, pairs)
        total = arrived.astype(jnp.float32) + own(step + 2)
    return total


def both_ways(forward, backward, axis, joined):
    count = lax.axis_size(axis)
    return jnp.concatenate(
        [
            ring_reduce_scatter(forward, axis, count, 1),
            ring_reduce_scatter(backward, axis, count, -1),
        ],
        axis=joined,
    )


def exchange_sum(parts, axis):
    moved = lax.all_to_all(parts.astype(jnp.bfloat16), axis, 0, 0, tiled=True)
    return jnp.sum(moved.astype(jnp.float32), axis=0)


def per_device(
    residual,
    query_new,
    key_new,
    value_new,
    key_cache,
    value_cache,
    lengths,
    norm_gain,
    router,
    routes,
    w_gate,
    w_up,
    w_down,
):
    env_count, step_count, slice_width = residual.shape
    local_experts, width, hidden_local = w_gate.shape
    experts = router.shape[1]
    topk = routes.shape[2]
    group_count = lax.axis_size("grp")
    tensor_count = lax.axis_size("tp")
    owner_count = lax.axis_size("ex")
    row_count = env_count * step_count
    state = residual.astype(jnp.float32) + attend(
        query_new, key_new, value_new, key_cache, value_cache, lengths
    )
    attended = state.astype(jnp.bfloat16)
    squares = jnp.sum(state * state, -1)
    scaled = state * norm_gain.astype(jnp.float32)
    partial_logits = jnp.einsum("esd,dx->esx", scaled, router, precision=lax.Precision.HIGHEST)
    squares, logits = lax.psum((squares, partial_logits), "tp")
    root_mean = jnp.sqrt(squares / width + 1e-05)[..., None]
    logits = logits / root_mean
    expert_ids = lax.broadcasted_iota(jnp.int32, (1, 1, 1, experts), 3)
    picked_logits = jnp.sum(
        jnp.where(routes[..., None] == expert_ids, logits[:, :, None, :], 0.0), -1
    )
    first_gate = 1.0 / (1.0 + jnp.exp(picked_logits[..., 1] - picked_logits[..., 0]))
    second_gate = 1.0 - first_gate
    flat_routes = routes.reshape(row_count * topk)
    expert_hits = (flat_routes[:, None] == lax.broadcasted_iota(jnp.int32, (1, experts), 1)).astype(
        jnp.int32
    )
    earlier = jnp.cumsum(expert_hits, axis=0) - expert_hits
    slot_ids = jnp.sum(earlier * expert_hits, axis=1)
    targets = flat_routes * CAP + slot_ids
    slot_table = lax.broadcasted_iota(jnp.int32, (1, experts * CAP), 1)
    placed = (
        (targets[:, None] == slot_table)
        .astype(jnp.bfloat16)
        .reshape(row_count, topk, experts * CAP)
    )
    sender = jnp.sum(placed, axis=1)
    packed = jnp.einsum(
        "rs,rd->sd",
        sender,
        attended.reshape(row_count, slice_width),
        preferred_element_type=jnp.float32,
    )
    outgoing = packed.astype(jnp.bfloat16).reshape(experts, CAP, slice_width)
    received = lax.all_to_all(outgoing, "ex", split_axis=0, concat_axis=0, tiled=True)
    received = received.reshape(1, owner_count, local_experts, CAP, slice_width)
    pieces = lax.all_gather(received, ("grp", "tp"), axis=0, tiled=True)

    pieces = pieces.reshape(
        group_count, tensor_count, owner_count, local_experts, CAP, slice_width
    ).astype(jnp.float32)
    gains = lax.all_gather(norm_gain, "tp", axis=0, tiled=True).astype(jnp.float32)
    slot_squares = jnp.sum(pieces * pieces, axis=(1, 5), keepdims=True)
    pieces = (pieces * gains.reshape(1, tensor_count, 1, 1, 1, slice_width)) / jnp.sqrt(
        slot_squares / width + 1e-05
    )
    pieces = pieces.astype(jnp.bfloat16)
    gate_split = w_gate.reshape(local_experts, tensor_count, slice_width, hidden_local)
    up_split = w_up.reshape(local_experts, tensor_count, slice_width, hidden_local)
    gate_sums = jnp.einsum(
        "gtajcd,jtdf->jgacf", pieces, gate_split, preferred_element_type=jnp.float32
    )
    up_sums = jnp.einsum("gtajcd,jtdf->jgacf", pieces, up_split, preferred_element_type=jnp.float32)
    hidden = (jax.nn.silu(gate_sums) * up_sums).astype(jnp.bfloat16)
    down_split = w_down.reshape(local_experts, hidden_local, tensor_count, slice_width)
    owner_half = owner_count // 2
    group_half = group_count // 2
    tensor_half = tensor_count // 2

    def down(rows, columns, spec):
        return jnp.einsum(spec, rows, columns, preferred_element_type=jnp.float32)

    z_rows = hidden[:, :, :owner_half]
    y_rows = hidden[:, :, owner_half:]
    z_first = both_ways(
        down(z_rows[:, :group_half], down_split, "jgacf,jftd->tgajcd"),
        down(z_rows[:, group_half:], down_split, "jgacf,jftd->tgajcd"),
        "tp",
        0,
    )
    y_first = both_ways(
        down(y_rows, down_split[:, :, :tensor_half], "jgacf,jftd->gtajcd"),
        down(y_rows, down_split[:, :, tensor_half:], "jgacf,jftd->gtajcd"),
        "grp",
        0,
    )
    z_done = exchange_sum(z_first, "grp")
    y_done = exchange_sum(y_first, "tp")
    summed = jnp.concatenate([z_done, y_done], axis=0)
    returned = lax.all_to_all(
        summed.astype(jnp.bfloat16), "ex", split_axis=0, concat_axis=0, tiled=True
    )
    returned = returned.reshape(experts * CAP, slice_width)
    picked_rows = jnp.einsum("rks,sd->rkd", placed, returned, preferred_element_type=jnp.float32)
    picked_rows = picked_rows.reshape(env_count, step_count, topk, slice_width)
    expert_mix = (
        first_gate[..., None] * picked_rows[:, :, 0] + second_gate[..., None] * picked_rows[:, :, 1]
    )
    return (attended, expert_mix.astype(jnp.bfloat16))


def solution(mesh):
    return jax.shard_map(
        per_device,
        mesh=mesh,
        in_specs=(
            P(("grp", "ex"), None, "tp"),
            P(("grp", "ex"), None, "tp"),
            P(("grp", "ex"), None, "tp"),
            P(("grp", "ex"), None, "tp"),
            P(("grp", "ex"), "tp", None, None),
            P(("grp", "ex"), "tp", None, None),
            P(("grp", "ex")),
            P("tp"),
            P("tp", None),
            P(("grp", "ex"), None, None),
            P("ex", None, ("grp", "tp")),
            P("ex", None, ("grp", "tp")),
            P("ex", ("grp", "tp"), None),
        ),
        out_specs=(P(("grp", "ex"), None, "tp"), P(("grp", "ex"), None, "tp")),
        check_vma=False,
    )
```

```python
import jax
import jax.numpy as jnp
from jax import lax
from jax.sharding import PartitionSpec as P

CAP = 16


def attend(query_new, key_new, value_new, key_cache, value_cache, lengths):
    env_count, step_count, feature_count = query_new.shape
    kv_count = key_cache.shape[1]
    context = key_cache.shape[2]
    head_dim = key_cache.shape[3]
    group_size = feature_count // (kv_count * head_dim)
    queries = query_new.reshape(env_count, step_count, kv_count, group_size, head_dim)
    keys_now = key_new.reshape(env_count, step_count, kv_count, head_dim)
    values_now = value_new.reshape(env_count, step_count, kv_count, head_dim)
    score_scale = head_dim ** (-0.5)
    cached = (
        jnp.einsum("eskgd,ekcd->eskgc", queries, key_cache, preferred_element_type=jnp.float32)
        * score_scale
    )
    fresh_scores = (
        jnp.einsum("eskgd,etkd->eskgt", queries, keys_now, preferred_element_type=jnp.float32)
        * score_scale
    )
    valid_mask = (lax.broadcasted_iota(jnp.int32, (env_count, context), 1) < lengths[:, None])[
        :, None, None, None, :
    ]
    causal = (
        lax.broadcasted_iota(jnp.int32, (step_count, step_count), 1)
        <= lax.broadcasted_iota(jnp.int32, (step_count, step_count), 0)
    )[None, :, None, None, :]
    cached = jnp.where(valid_mask, cached, -1e30)
    fresh_scores = jnp.where(causal, fresh_scores, -1e30)
    row_top = jnp.maximum(jnp.max(cached, -1), jnp.max(fresh_scores, -1))[..., None]
    weight_cached = jnp.where(valid_mask, jnp.exp(cached - row_top), 0.0)
    weight_fresh = jnp.where(causal, jnp.exp(fresh_scores - row_top), 0.0)
    row_total = (jnp.sum(weight_cached, -1) + jnp.sum(weight_fresh, -1))[..., None]
    probs_cached = (weight_cached / row_total).astype(jnp.bfloat16)
    probs_fresh = (weight_fresh / row_total).astype(jnp.bfloat16)
    heads_out = jnp.einsum(
        "eskgc,ekcd->eskgd", probs_cached, value_cache, preferred_element_type=jnp.float32
    )
    heads_out = heads_out + jnp.einsum(
        "eskgt,etkd->eskgd", probs_fresh, values_now, preferred_element_type=jnp.float32
    )
    return heads_out.reshape(env_count, step_count, feature_count)


def ring_reduce_scatter(parts, axis, count, direction):
    me = lax.axis_index(axis)
    pairs = [(j, (j + direction) % count) for j in range(count)]

    def own(offset):
        chunk = (me - direction * offset) % count
        return lax.dynamic_index_in_dim(parts, chunk, 0, keepdims=False)

    total = own(1)
    for step in range(count - 1):
        arrived = lax.ppermute(total.astype(jnp.bfloat16), axis, pairs)
        total = arrived.astype(jnp.float32) + own(step + 2)
    return total


def both_ways(forward, backward, axis, joined):
    count = lax.axis_size(axis)
    return jnp.concatenate(
        [
            ring_reduce_scatter(forward, axis, count, 1),
            ring_reduce_scatter(backward, axis, count, -1),
        ],
        axis=joined,
    )


def exchange_sum(parts, axis):
    moved = lax.all_to_all(parts.astype(jnp.bfloat16), axis, 0, 0, tiled=True)
    return jnp.sum(moved.astype(jnp.float32), axis=0)


def per_device(
    residual,
    query_new,
    key_new,
    value_new,
    key_cache,
    value_cache,
    lengths,
    norm_gain,
    router,
    routes,
    w_gate,
    w_up,
    w_down,
):
    env_count, step_count, slice_width = residual.shape
    local_experts, width, hidden_local = w_gate.shape
    experts = router.shape[1]
    topk = routes.shape[2]
    group_count = lax.axis_size("grp")
    tensor_count = lax.axis_size("tp")
    owner_count = lax.axis_size("ex")
    row_count = env_count * step_count
    state = residual.astype(jnp.float32) + attend(
        query_new, key_new, value_new, key_cache, value_cache, lengths
    )
    attended = state.astype(jnp.bfloat16)
    squares = jnp.sum(state * state, -1)
    scaled = state * norm_gain.astype(jnp.float32)
    partial_logits = jnp.einsum("esd,dx->esx", scaled, router, precision=lax.Precision.HIGHEST)
    stats = jnp.concatenate([squares[..., None], partial_logits], axis=-1)
    stats_high = stats.astype(jnp.bfloat16)
    stats_low = (stats - stats_high.astype(jnp.float32)).astype(jnp.bfloat16)
    stat_count = stats.size
    extras = jnp.zeros((2, slice_width), jnp.bfloat16)
    extras = extras.at[0].set(norm_gain)
    extras = extras.at[1, :stat_count].set(stats_high.reshape(stat_count))
    extras = extras.at[1, stat_count : 2 * stat_count].set(stats_low.reshape(stat_count))
    flat_routes = routes.reshape(row_count * topk)
    expert_hits = (flat_routes[:, None] == lax.broadcasted_iota(jnp.int32, (1, experts), 1)).astype(
        jnp.int32
    )
    earlier = jnp.cumsum(expert_hits, axis=0) - expert_hits
    slot_ids = jnp.sum(earlier * expert_hits, axis=1)
    targets = flat_routes * CAP + slot_ids
    slot_table = lax.broadcasted_iota(jnp.int32, (1, experts * CAP), 1)
    placed = (
        (targets[:, None] == slot_table)
        .astype(jnp.bfloat16)
        .reshape(row_count, topk, experts * CAP)
    )
    sender = jnp.sum(placed, axis=1)
    packed = jnp.einsum(
        "rs,rd->sd",
        sender,
        attended.reshape(row_count, slice_width),
        preferred_element_type=jnp.float32,
    )
    outgoing = packed.astype(jnp.bfloat16).reshape(experts, CAP, slice_width)
    received = lax.all_to_all(outgoing, "ex", split_axis=0, concat_axis=0, tiled=True)
    block_rows = owner_count * local_experts * CAP
    payload = jnp.concatenate([received.reshape(block_rows, slice_width), extras], axis=0)
    gathered = lax.all_gather(payload[None], ("grp", "tp"), axis=0, tiled=True)
    pieces = gathered[:, :block_rows]
    gain_rows = gathered[:, block_rows]
    stat_rows = gathered[:, block_rows + 1].reshape(group_count, tensor_count, slice_width)
    stat_rows = lax.dynamic_index_in_dim(stat_rows, lax.axis_index("grp"), 0, keepdims=False)
    stat_rows = stat_rows.astype(jnp.float32)
    stats = jnp.sum(stat_rows[:, :stat_count] + stat_rows[:, stat_count : 2 * stat_count], 0)
    stats = stats.reshape(env_count, step_count, experts + 1)
    squares, logits = stats[..., 0], stats[..., 1:]
    root_mean = jnp.sqrt(squares / width + 1e-05)[..., None]
    logits = logits / root_mean
    expert_ids = lax.broadcasted_iota(jnp.int32, (1, 1, 1, experts), 3)
    picked_logits = jnp.sum(
        jnp.where(routes[..., None] == expert_ids, logits[:, :, None, :], 0.0), -1
    )
    first_gate = 1.0 / (1.0 + jnp.exp(picked_logits[..., 1] - picked_logits[..., 0]))
    second_gate = 1.0 - first_gate

    pieces = pieces.reshape(
        group_count, tensor_count, owner_count, local_experts, CAP, slice_width
    ).astype(jnp.float32)
    gains = gain_rows.reshape(group_count, width)[0].astype(jnp.float32)
    slot_squares = jnp.sum(pieces * pieces, axis=(1, 5), keepdims=True)
    pieces = (pieces * gains.reshape(1, tensor_count, 1, 1, 1, slice_width)) / jnp.sqrt(
        slot_squares / width + 1e-05
    )
    pieces = pieces.astype(jnp.bfloat16)
    gate_split = w_gate.reshape(local_experts, tensor_count, slice_width, hidden_local)
    up_split = w_up.reshape(local_experts, tensor_count, slice_width, hidden_local)
    gate_sums = jnp.einsum(
        "gtajcd,jtdf->jgacf", pieces, gate_split, preferred_element_type=jnp.float32
    )
    up_sums = jnp.einsum("gtajcd,jtdf->jgacf", pieces, up_split, preferred_element_type=jnp.float32)
    hidden = (jax.nn.silu(gate_sums) * up_sums).astype(jnp.bfloat16)
    down_split = w_down.reshape(local_experts, hidden_local, tensor_count, slice_width)
    owner_half = owner_count // 2
    group_half = group_count // 2
    tensor_half = tensor_count // 2

    def down(rows, columns, spec):
        return jnp.einsum(spec, rows, columns, preferred_element_type=jnp.float32)

    z_rows = hidden[:, :, :owner_half]
    y_rows = hidden[:, :, owner_half:]
    z_first = both_ways(
        down(z_rows[:, :group_half], down_split, "jgacf,jftd->tgajcd"),
        down(z_rows[:, group_half:], down_split, "jgacf,jftd->tgajcd"),
        "tp",
        0,
    )
    y_first = both_ways(
        down(y_rows, down_split[:, :, :tensor_half], "jgacf,jftd->gtajcd"),
        down(y_rows, down_split[:, :, tensor_half:], "jgacf,jftd->gtajcd"),
        "grp",
        0,
    )
    z_done = exchange_sum(z_first, "grp")
    y_done = exchange_sum(y_first, "tp")
    summed = jnp.concatenate([z_done, y_done], axis=0)
    returned = lax.all_to_all(
        summed.astype(jnp.bfloat16), "ex", split_axis=0, concat_axis=0, tiled=True
    )
    returned = returned.reshape(experts * CAP, slice_width)
    picked_rows = jnp.einsum("rks,sd->rkd", placed, returned, preferred_element_type=jnp.float32)
    picked_rows = picked_rows.reshape(env_count, step_count, topk, slice_width)
    expert_mix = (
        first_gate[..., None] * picked_rows[:, :, 0] + second_gate[..., None] * picked_rows[:, :, 1]
    )
    return (attended, expert_mix.astype(jnp.bfloat16))


def solution(mesh):
    return jax.shard_map(
        per_device,
        mesh=mesh,
        in_specs=(
            P(("grp", "ex"), None, "tp"),
            P(("grp", "ex"), None, "tp"),
            P(("grp", "ex"), None, "tp"),
            P(("grp", "ex"), None, "tp"),
            P(("grp", "ex"), "tp", None, None),
            P(("grp", "ex"), "tp", None, None),
            P(("grp", "ex")),
            P("tp"),
            P("tp", None),
            P(("grp", "ex"), None, None),
            P("ex", None, ("grp", "tp")),
            P("ex", None, ("grp", "tp")),
            P("ex", ("grp", "tp"), None),
        ),
        out_specs=(P(("grp", "ex"), None, "tp"), P(("grp", "ex"), None, "tp")),
        check_vma=False,
    )
```

```python
import jax
import jax.numpy as jnp
from jax import lax
from jax.sharding import PartitionSpec as P

CAP = 16


def attend(query_new, key_new, value_new, key_cache, value_cache, lengths):
    env_count, step_count, feature_count = query_new.shape
    kv_count = key_cache.shape[1]
    context = key_cache.shape[2]
    head_dim = key_cache.shape[3]
    group_size = feature_count // (kv_count * head_dim)
    queries = query_new.reshape(env_count, step_count, kv_count, group_size, head_dim)
    keys_now = key_new.reshape(env_count, step_count, kv_count, head_dim)
    values_now = value_new.reshape(env_count, step_count, kv_count, head_dim)
    score_scale = head_dim ** (-0.5)
    cached = (
        jnp.einsum("eskgd,ekcd->eskgc", queries, key_cache, preferred_element_type=jnp.float32)
        * score_scale
    )
    fresh_scores = (
        jnp.einsum("eskgd,etkd->eskgt", queries, keys_now, preferred_element_type=jnp.float32)
        * score_scale
    )
    valid_mask = (lax.broadcasted_iota(jnp.int32, (env_count, context), 1) < lengths[:, None])[
        :, None, None, None, :
    ]
    causal = (
        lax.broadcasted_iota(jnp.int32, (step_count, step_count), 1)
        <= lax.broadcasted_iota(jnp.int32, (step_count, step_count), 0)
    )[None, :, None, None, :]
    cached = jnp.where(valid_mask, cached, -1e30)
    fresh_scores = jnp.where(causal, fresh_scores, -1e30)
    row_top = jnp.maximum(jnp.max(cached, -1), jnp.max(fresh_scores, -1))[..., None]
    weight_cached = jnp.where(valid_mask, jnp.exp(cached - row_top), 0.0)
    weight_fresh = jnp.where(causal, jnp.exp(fresh_scores - row_top), 0.0)
    row_total = (jnp.sum(weight_cached, -1) + jnp.sum(weight_fresh, -1))[..., None]
    probs_cached = (weight_cached / row_total).astype(jnp.bfloat16)
    probs_fresh = (weight_fresh / row_total).astype(jnp.bfloat16)
    heads_out = jnp.einsum(
        "eskgc,ekcd->eskgd", probs_cached, value_cache, preferred_element_type=jnp.float32
    )
    heads_out = heads_out + jnp.einsum(
        "eskgt,etkd->eskgd", probs_fresh, values_now, preferred_element_type=jnp.float32
    )
    return heads_out.reshape(env_count, step_count, feature_count)


def ring_reduce_scatter(parts, axis, count, direction):
    me = lax.axis_index(axis)
    pairs = [(j, (j + direction) % count) for j in range(count)]

    def own(offset):
        chunk = (me - direction * offset) % count
        return lax.dynamic_index_in_dim(parts, chunk, 0, keepdims=False)

    total = own(1)
    for step in range(count - 1):
        arrived = lax.ppermute(total.astype(jnp.bfloat16), axis, pairs)
        total = arrived.astype(jnp.float32) + own(step + 2)
    return total


def both_ways(forward, backward, axis, joined):
    count = lax.axis_size(axis)
    return jnp.concatenate(
        [
            ring_reduce_scatter(forward, axis, count, 1),
            ring_reduce_scatter(backward, axis, count, -1),
        ],
        axis=joined,
    )


def exchange_sum(parts, axis):
    moved = lax.all_to_all(parts.astype(jnp.bfloat16), axis, 0, 0, tiled=True)
    return jnp.sum(moved.astype(jnp.float32), axis=0)


def per_device(
    residual,
    query_new,
    key_new,
    value_new,
    key_cache,
    value_cache,
    lengths,
    norm_gain,
    router,
    routes,
    w_gate,
    w_up,
    w_down,
):
    env_count, step_count, slice_width = residual.shape
    local_experts, width, hidden_local = w_gate.shape
    experts = router.shape[1]
    topk = routes.shape[2]
    group_count = lax.axis_size("grp")
    tensor_count = lax.axis_size("tp")
    owner_count = lax.axis_size("ex")
    row_count = env_count * step_count
    state = residual.astype(jnp.float32) + attend(
        query_new, key_new, value_new, key_cache, value_cache, lengths
    )
    attended = state.astype(jnp.bfloat16)
    squares = jnp.sum(state * state, -1)
    scaled = state * norm_gain.astype(jnp.float32)
    partial_logits = jnp.einsum("esd,dx->esx", scaled, router, precision=lax.Precision.HIGHEST)
    stats = jnp.concatenate([squares[..., None], partial_logits], axis=-1)
    stats_high = stats.astype(jnp.bfloat16)
    stats_low = (stats - stats_high.astype(jnp.float32)).astype(jnp.bfloat16)
    stat_count = stats.size
    extras = jnp.zeros((2, slice_width), jnp.bfloat16)
    extras = extras.at[0].set(norm_gain)
    extras = extras.at[1, :stat_count].set(stats_high.reshape(stat_count))
    extras = extras.at[1, stat_count : 2 * stat_count].set(stats_low.reshape(stat_count))
    flat_routes = routes.reshape(row_count * topk)
    expert_hits = (flat_routes[:, None] == lax.broadcasted_iota(jnp.int32, (1, experts), 1)).astype(
        jnp.int32
    )
    earlier = jnp.cumsum(expert_hits, axis=0) - expert_hits
    slot_ids = jnp.sum(earlier * expert_hits, axis=1)
    targets = flat_routes * CAP + slot_ids
    slot_table = lax.broadcasted_iota(jnp.int32, (1, experts * CAP), 1)
    placed = (
        (targets[:, None] == slot_table)
        .astype(jnp.bfloat16)
        .reshape(row_count, topk, experts * CAP)
    )
    sender = jnp.sum(placed, axis=1)
    packed = jnp.einsum(
        "rs,rd->sd",
        sender,
        attended.reshape(row_count, slice_width),
        preferred_element_type=jnp.float32,
    )
    outgoing = packed.astype(jnp.bfloat16).reshape(experts, CAP, slice_width)
    received = lax.all_to_all(outgoing, "ex", split_axis=0, concat_axis=0, tiled=True)
    block_rows = owner_count * local_experts * CAP
    payload = jnp.concatenate([received.reshape(block_rows, slice_width), extras], axis=0)
    gathered = lax.all_gather(payload[None], ("grp", "tp"), axis=0, tiled=True)
    stat_rows = gathered[:, block_rows + 1].reshape(group_count, tensor_count, slice_width)
    stat_rows = lax.dynamic_index_in_dim(stat_rows, lax.axis_index("grp"), 0, keepdims=False)
    stat_rows = stat_rows.astype(jnp.float32)
    stats = jnp.sum(stat_rows[:, :stat_count] + stat_rows[:, stat_count : 2 * stat_count], 0)
    stats = stats.reshape(env_count, step_count, experts + 1)
    squares, logits = stats[..., 0], stats[..., 1:]
    root_mean = jnp.sqrt(squares / width + 1e-05)[..., None]
    logits = logits / root_mean
    expert_ids = lax.broadcasted_iota(jnp.int32, (1, 1, 1, experts), 3)
    picked_logits = jnp.sum(
        jnp.where(routes[..., None] == expert_ids, logits[:, :, None, :], 0.0), -1
    )
    first_gate = 1.0 / (1.0 + jnp.exp(picked_logits[..., 1] - picked_logits[..., 0]))
    second_gate = 1.0 - first_gate

    rows = gathered.reshape(group_count, tensor_count, block_rows + 2, slice_width)
    gains = rows[0, :, block_rows].astype(jnp.float32)
    wide = rows.astype(jnp.float32)
    slot_scale = jnp.sqrt(jnp.sum(wide * wide, axis=(1, 3)) / width + 1e-05)[..., None]
    scaled_rows = (wide * gains[None, :, None, :]).astype(jnp.bfloat16)

    def expert_in(weights):
        split = weights.reshape(tensor_count, slice_width, hidden_local)
        sums = jnp.einsum("gtrd,tdf->grf", scaled_rows, split, preferred_element_type=jnp.float32)
        sums = (sums / slot_scale)[:, :block_rows]
        return sums.reshape(local_experts, group_count, owner_count, CAP, hidden_local)

    gate_sums = expert_in(w_gate)
    up_sums = expert_in(w_up)
    hidden = (jax.nn.silu(gate_sums) * up_sums).astype(jnp.bfloat16)
    down_split = w_down.reshape(local_experts, hidden_local, tensor_count, slice_width)
    owner_half = owner_count // 2
    group_half = group_count // 2
    tensor_half = tensor_count // 2

    def down(rows, columns, spec):
        return jnp.einsum(spec, rows, columns, preferred_element_type=jnp.float32)

    z_rows = hidden[:, :, :owner_half]
    y_rows = hidden[:, :, owner_half:]
    z_first = both_ways(
        down(z_rows[:, :group_half], down_split, "jgacf,jftd->tgajcd"),
        down(z_rows[:, group_half:], down_split, "jgacf,jftd->tgajcd"),
        "tp",
        0,
    )
    y_first = both_ways(
        down(y_rows, down_split[:, :, :tensor_half], "jgacf,jftd->gtajcd"),
        down(y_rows, down_split[:, :, tensor_half:], "jgacf,jftd->gtajcd"),
        "grp",
        0,
    )
    z_done = exchange_sum(z_first, "grp")
    y_done = exchange_sum(y_first, "tp")
    summed = jnp.concatenate([z_done, y_done], axis=0)
    returned = lax.all_to_all(
        summed.astype(jnp.bfloat16), "ex", split_axis=0, concat_axis=0, tiled=True
    )
    returned = returned.reshape(experts * CAP, slice_width)
    picked_rows = jnp.einsum("rks,sd->rkd", placed, returned, preferred_element_type=jnp.float32)
    picked_rows = picked_rows.reshape(env_count, step_count, topk, slice_width)
    expert_mix = (
        first_gate[..., None] * picked_rows[:, :, 0] + second_gate[..., None] * picked_rows[:, :, 1]
    )
    return (attended, expert_mix.astype(jnp.bfloat16))


def solution(mesh):
    return jax.shard_map(
        per_device,
        mesh=mesh,
        in_specs=(
            P(("grp", "ex"), None, "tp"),
            P(("grp", "ex"), None, "tp"),
            P(("grp", "ex"), None, "tp"),
            P(("grp", "ex"), None, "tp"),
            P(("grp", "ex"), "tp", None, None),
            P(("grp", "ex"), "tp", None, None),
            P(("grp", "ex")),
            P("tp"),
            P("tp", None),
            P(("grp", "ex"), None, None),
            P("ex", None, ("grp", "tp")),
            P("ex", None, ("grp", "tp")),
            P("ex", ("grp", "tp"), None),
        ),
        out_specs=(P(("grp", "ex"), None, "tp"), P(("grp", "ex"), None, "tp")),
        check_vma=False,
    )
```

```python
import jax
import jax.numpy as jnp
from jax import lax
from jax.sharding import PartitionSpec as P

CAP = 16


def attend(query_new, key_new, value_new, key_cache, value_cache, lengths):
    env_count, step_count, feature_count = query_new.shape
    kv_count = key_cache.shape[1]
    context = key_cache.shape[2]
    head_dim = key_cache.shape[3]
    group_size = feature_count // (kv_count * head_dim)
    queries = query_new.reshape(env_count, step_count, kv_count, group_size, head_dim)
    keys_now = key_new.reshape(env_count, step_count, kv_count, head_dim)
    values_now = value_new.reshape(env_count, step_count, kv_count, head_dim)
    score_scale = head_dim ** (-0.5)
    cached = (
        jnp.einsum("eskgd,ekcd->eskgc", queries, key_cache, preferred_element_type=jnp.float32)
        * score_scale
    )
    fresh_scores = (
        jnp.einsum("eskgd,etkd->eskgt", queries, keys_now, preferred_element_type=jnp.float32)
        * score_scale
    )
    valid_mask = (lax.broadcasted_iota(jnp.int32, (env_count, context), 1) < lengths[:, None])[
        :, None, None, None, :
    ]
    causal = (
        lax.broadcasted_iota(jnp.int32, (step_count, step_count), 1)
        <= lax.broadcasted_iota(jnp.int32, (step_count, step_count), 0)
    )[None, :, None, None, :]
    cached = jnp.where(valid_mask, cached, -1e30)
    fresh_scores = jnp.where(causal, fresh_scores, -1e30)
    row_top = jnp.maximum(jnp.max(cached, -1), jnp.max(fresh_scores, -1))[..., None]
    weight_cached = jnp.where(valid_mask, jnp.exp(cached - row_top), 0.0)
    weight_fresh = jnp.where(causal, jnp.exp(fresh_scores - row_top), 0.0)
    row_total = (jnp.sum(weight_cached, -1) + jnp.sum(weight_fresh, -1))[..., None]
    probs_cached = (weight_cached / row_total).astype(jnp.bfloat16)
    probs_fresh = (weight_fresh / row_total).astype(jnp.bfloat16)
    heads_out = jnp.einsum(
        "eskgc,ekcd->eskgd", probs_cached, value_cache, preferred_element_type=jnp.float32
    )
    heads_out = heads_out + jnp.einsum(
        "eskgt,etkd->eskgd", probs_fresh, values_now, preferred_element_type=jnp.float32
    )
    return heads_out.reshape(env_count, step_count, feature_count)


def ring_reduce_scatter(parts, axis, count, direction):
    me = lax.axis_index(axis)
    pairs = [(j, (j + direction) % count) for j in range(count)]

    def own(offset):
        chunk = (me - direction * offset) % count
        return lax.dynamic_index_in_dim(parts, chunk, 0, keepdims=False)

    total = own(1)
    for step in range(count - 1):
        arrived = lax.ppermute(total.astype(jnp.bfloat16), axis, pairs)
        total = arrived.astype(jnp.float32) + own(step + 2)
    return total


def both_ways(forward, backward, axis, joined):
    count = lax.axis_size(axis)
    return jnp.concatenate(
        [
            ring_reduce_scatter(forward, axis, count, 1),
            ring_reduce_scatter(backward, axis, count, -1),
        ],
        axis=joined,
    )


def exchange_sum(parts, axis):
    moved = lax.all_to_all(parts.astype(jnp.bfloat16), axis, 0, 0, tiled=True)
    return jnp.sum(moved.astype(jnp.float32), axis=0)


def per_device(
    residual,
    query_new,
    key_new,
    value_new,
    key_cache,
    value_cache,
    lengths,
    norm_gain,
    router,
    routes,
    w_gate,
    w_up,
    w_down,
):
    env_count, step_count, slice_width = residual.shape
    local_experts, width, hidden_local = w_gate.shape
    experts = router.shape[1]
    topk = routes.shape[2]
    group_count = lax.axis_size("grp")
    tensor_count = lax.axis_size("tp")
    owner_count = lax.axis_size("ex")
    row_count = env_count * step_count
    state = residual.astype(jnp.float32) + attend(
        query_new, key_new, value_new, key_cache, value_cache, lengths
    )
    attended = state.astype(jnp.bfloat16)
    squares = jnp.sum(state * state, -1)
    scaled = state * norm_gain.astype(jnp.float32)
    partial_logits = jnp.einsum("esd,dx->esx", scaled, router, precision=lax.Precision.HIGHEST)
    stats = jnp.concatenate([squares[..., None], partial_logits], axis=-1)
    stats_high = stats.astype(jnp.bfloat16)
    stats_low = (stats - stats_high.astype(jnp.float32)).astype(jnp.bfloat16)
    stat_count = stats.size
    extras = jnp.zeros((2, slice_width), jnp.bfloat16)
    extras = extras.at[0].set(norm_gain)
    extras = extras.at[1, :stat_count].set(stats_high.reshape(stat_count))
    extras = extras.at[1, stat_count : 2 * stat_count].set(stats_low.reshape(stat_count))
    flat_routes = routes.reshape(row_count * topk)
    expert_hits = (flat_routes[:, None] == lax.broadcasted_iota(jnp.int32, (1, experts), 1)).astype(
        jnp.int32
    )
    earlier = jnp.cumsum(expert_hits, axis=0) - expert_hits
    slot_ids = jnp.sum(earlier * expert_hits, axis=1)
    targets = flat_routes * CAP + slot_ids
    slot_table = lax.broadcasted_iota(jnp.int32, (1, experts * CAP), 1)
    placed = (
        (targets[:, None] == slot_table)
        .astype(jnp.bfloat16)
        .reshape(row_count, topk, experts * CAP)
    )
    sender = jnp.sum(placed, axis=1)
    packed = jnp.einsum(
        "rs,rd->sd",
        sender,
        attended.reshape(row_count, slice_width),
        preferred_element_type=jnp.float32,
    )
    outgoing = packed.astype(jnp.bfloat16).reshape(experts, CAP, slice_width)
    received = lax.all_to_all(outgoing, "ex", split_axis=0, concat_axis=0, tiled=True)
    block_rows = owner_count * local_experts * CAP
    payload = jnp.concatenate([received.reshape(block_rows, slice_width), extras], axis=0)
    gathered = lax.all_gather(payload[None], "tp", axis=0, tiled=True)
    gathered = lax.all_gather(gathered, "grp", axis=0, tiled=True)
    stat_rows = gathered[:, block_rows + 1].reshape(group_count, tensor_count, slice_width)
    stat_rows = lax.dynamic_index_in_dim(stat_rows, lax.axis_index("grp"), 0, keepdims=False)
    stat_rows = stat_rows.astype(jnp.float32)
    stats = jnp.sum(stat_rows[:, :stat_count] + stat_rows[:, stat_count : 2 * stat_count], 0)
    stats = stats.reshape(env_count, step_count, experts + 1)
    squares, logits = stats[..., 0], stats[..., 1:]
    root_mean = jnp.sqrt(squares / width + 1e-05)[..., None]
    logits = logits / root_mean
    expert_ids = lax.broadcasted_iota(jnp.int32, (1, 1, 1, experts), 3)
    picked_logits = jnp.sum(
        jnp.where(routes[..., None] == expert_ids, logits[:, :, None, :], 0.0), -1
    )
    first_gate = 1.0 / (1.0 + jnp.exp(picked_logits[..., 1] - picked_logits[..., 0]))
    second_gate = 1.0 - first_gate

    rows = gathered.reshape(group_count, tensor_count, block_rows + 2, slice_width)
    gains = rows[0, :, block_rows].astype(jnp.float32)
    wide = rows.astype(jnp.float32)
    slot_scale = jnp.sqrt(jnp.sum(wide * wide, axis=(1, 3)) / width + 1e-05)[..., None]
    scaled_rows = (wide * gains[None, :, None, :]).astype(jnp.bfloat16)

    def expert_in(weights):
        split = weights.reshape(tensor_count, slice_width, hidden_local)
        sums = jnp.einsum("gtrd,tdf->grf", scaled_rows, split, preferred_element_type=jnp.float32)
        sums = (sums / slot_scale)[:, :block_rows]
        return sums.reshape(local_experts, group_count, owner_count, CAP, hidden_local)

    gate_sums = expert_in(w_gate)
    up_sums = expert_in(w_up)
    hidden = (jax.nn.silu(gate_sums) * up_sums).astype(jnp.bfloat16)
    down_split = w_down.reshape(local_experts, hidden_local, tensor_count, slice_width)
    owner_half = owner_count // 2
    group_half = group_count // 2
    tensor_half = tensor_count // 2

    def down(rows, columns, spec):
        return jnp.einsum(spec, rows, columns, preferred_element_type=jnp.float32)

    z_rows = hidden[:, :, :owner_half]
    y_rows = hidden[:, :, owner_half:]
    z_first = both_ways(
        down(z_rows[:, :group_half], down_split, "jgacf,jftd->tgajcd"),
        down(z_rows[:, group_half:], down_split, "jgacf,jftd->tgajcd"),
        "tp",
        0,
    )
    y_first = both_ways(
        down(y_rows, down_split[:, :, :tensor_half], "jgacf,jftd->gtajcd"),
        down(y_rows, down_split[:, :, tensor_half:], "jgacf,jftd->gtajcd"),
        "grp",
        0,
    )
    z_done = exchange_sum(z_first, "grp")
    y_done = exchange_sum(y_first, "tp")
    summed = jnp.concatenate([z_done, y_done], axis=0)
    returned = lax.all_to_all(
        summed.astype(jnp.bfloat16), "ex", split_axis=0, concat_axis=0, tiled=True
    )
    returned = returned.reshape(experts * CAP, slice_width)
    picked_rows = jnp.einsum("rks,sd->rkd", placed, returned, preferred_element_type=jnp.float32)
    picked_rows = picked_rows.reshape(env_count, step_count, topk, slice_width)
    expert_mix = (
        first_gate[..., None] * picked_rows[:, :, 0] + second_gate[..., None] * picked_rows[:, :, 1]
    )
    return (attended, expert_mix.astype(jnp.bfloat16))


def solution(mesh):
    return jax.shard_map(
        per_device,
        mesh=mesh,
        in_specs=(
            P(("grp", "ex"), None, "tp"),
            P(("grp", "ex"), None, "tp"),
            P(("grp", "ex"), None, "tp"),
            P(("grp", "ex"), None, "tp"),
            P(("grp", "ex"), "tp", None, None),
            P(("grp", "ex"), "tp", None, None),
            P(("grp", "ex")),
            P("tp"),
            P("tp", None),
            P(("grp", "ex"), None, None),
            P("ex", None, ("grp", "tp")),
            P("ex", None, ("grp", "tp")),
            P("ex", ("grp", "tp"), None),
        ),
        out_specs=(P(("grp", "ex"), None, "tp"), P(("grp", "ex"), None, "tp")),
        check_vma=False,
    )
```

```python
import jax
import jax.numpy as jnp
from jax import lax
from jax.sharding import PartitionSpec as P

CAP = 16


def attend(query_new, key_new, value_new, key_cache, value_cache, lengths):
    env_count, step_count, feature_count = query_new.shape
    kv_count = key_cache.shape[1]
    context = key_cache.shape[2]
    head_dim = key_cache.shape[3]
    group_size = feature_count // (kv_count * head_dim)
    queries = query_new.reshape(env_count, step_count, kv_count, group_size, head_dim)
    keys_now = key_new.reshape(env_count, step_count, kv_count, head_dim)
    values_now = value_new.reshape(env_count, step_count, kv_count, head_dim)
    score_scale = head_dim ** (-0.5)
    cached = (
        jnp.einsum("eskgd,ekcd->eskgc", queries, key_cache, preferred_element_type=jnp.float32)
        * score_scale
    )
    fresh_scores = (
        jnp.einsum("eskgd,etkd->eskgt", queries, keys_now, preferred_element_type=jnp.float32)
        * score_scale
    )
    valid_mask = (lax.broadcasted_iota(jnp.int32, (env_count, context), 1) < lengths[:, None])[
        :, None, None, None, :
    ]
    causal = (
        lax.broadcasted_iota(jnp.int32, (step_count, step_count), 1)
        <= lax.broadcasted_iota(jnp.int32, (step_count, step_count), 0)
    )[None, :, None, None, :]
    cached = jnp.where(valid_mask, cached, -1e30)
    fresh_scores = jnp.where(causal, fresh_scores, -1e30)
    row_top = jnp.maximum(jnp.max(cached, -1), jnp.max(fresh_scores, -1))[..., None]
    weight_cached = jnp.where(valid_mask, jnp.exp(cached - row_top), 0.0)
    weight_fresh = jnp.where(causal, jnp.exp(fresh_scores - row_top), 0.0)
    row_total = (jnp.sum(weight_cached, -1) + jnp.sum(weight_fresh, -1))[..., None]
    probs_cached = (weight_cached / row_total).astype(jnp.bfloat16)
    probs_fresh = (weight_fresh / row_total).astype(jnp.bfloat16)
    heads_out = jnp.einsum(
        "eskgc,ekcd->eskgd", probs_cached, value_cache, preferred_element_type=jnp.float32
    )
    heads_out = heads_out + jnp.einsum(
        "eskgt,etkd->eskgd", probs_fresh, values_now, preferred_element_type=jnp.float32
    )
    return heads_out.reshape(env_count, step_count, feature_count)


def ring_reduce_scatter(parts, axis, count, direction):
    me = lax.axis_index(axis)
    pairs = [(j, (j + direction) % count) for j in range(count)]

    def own(offset):
        chunk = (me - direction * offset) % count
        return lax.dynamic_index_in_dim(parts, chunk, 0, keepdims=False)

    total = own(1)
    for step in range(count - 1):
        arrived = lax.ppermute(total.astype(jnp.bfloat16), axis, pairs)
        total = arrived.astype(jnp.float32) + own(step + 2)
    return total


def both_ways(forward, backward, axis, joined):
    count = lax.axis_size(axis)
    return jnp.concatenate(
        [
            ring_reduce_scatter(forward, axis, count, 1),
            ring_reduce_scatter(backward, axis, count, -1),
        ],
        axis=joined,
    )


def exchange_sum(parts, axis):
    moved = lax.all_to_all(parts.astype(jnp.bfloat16), axis, 0, 0, tiled=True)
    return jnp.sum(moved.astype(jnp.float32), axis=0)


def per_device(
    residual,
    query_new,
    key_new,
    value_new,
    key_cache,
    value_cache,
    lengths,
    norm_gain,
    router,
    routes,
    w_gate,
    w_up,
    w_down,
):
    env_count, step_count, slice_width = residual.shape
    local_experts, width, hidden_local = w_gate.shape
    experts = router.shape[1]
    topk = routes.shape[2]
    group_count = lax.axis_size("grp")
    tensor_count = lax.axis_size("tp")
    owner_count = lax.axis_size("ex")
    row_count = env_count * step_count
    state = residual.astype(jnp.float32) + attend(
        query_new, key_new, value_new, key_cache, value_cache, lengths
    )
    attended = state.astype(jnp.bfloat16)
    squares = jnp.sum(state * state, -1)
    scaled = state * norm_gain.astype(jnp.float32)
    partial_logits = jnp.einsum("esd,dx->esx", scaled, router, precision=lax.Precision.HIGHEST)
    stats = jnp.concatenate([squares[..., None], partial_logits], axis=-1)
    stats_high = stats.astype(jnp.bfloat16)
    stats_low = (stats - stats_high.astype(jnp.float32)).astype(jnp.bfloat16)
    stat_count = stats.size
    extras = jnp.zeros((2, slice_width), jnp.bfloat16)
    extras = extras.at[0].set(norm_gain)
    extras = extras.at[1, :stat_count].set(stats_high.reshape(stat_count))
    extras = extras.at[1, stat_count : 2 * stat_count].set(stats_low.reshape(stat_count))
    flat_routes = routes.reshape(row_count * topk)
    expert_hits = (flat_routes[:, None] == lax.broadcasted_iota(jnp.int32, (1, experts), 1)).astype(
        jnp.int32
    )
    earlier = jnp.cumsum(expert_hits, axis=0) - expert_hits
    slot_ids = jnp.sum(earlier * expert_hits, axis=1)
    targets = flat_routes * CAP + slot_ids
    slot_table = lax.broadcasted_iota(jnp.int32, (1, experts * CAP), 1)
    placed = (
        (targets[:, None] == slot_table)
        .astype(jnp.bfloat16)
        .reshape(row_count, topk, experts * CAP)
    )
    sender = jnp.sum(placed, axis=1)
    packed = jnp.einsum(
        "rs,rd->sd",
        sender,
        attended.reshape(row_count, slice_width),
        preferred_element_type=jnp.float32,
    )
    outgoing = packed.astype(jnp.bfloat16).reshape(experts, CAP, slice_width)
    received = lax.all_to_all(outgoing, "ex", split_axis=0, concat_axis=0, tiled=True)
    block_rows = owner_count * local_experts * CAP
    payload = jnp.concatenate([received.reshape(block_rows, slice_width), extras], axis=0)
    gathered = lax.all_gather(payload[None], ("grp", "tp"), axis=0, tiled=True)
    stat_rows = gathered[:, block_rows + 1].reshape(group_count, tensor_count, slice_width)
    stat_rows = lax.dynamic_index_in_dim(stat_rows, lax.axis_index("grp"), 0, keepdims=False)
    stat_rows = stat_rows.astype(jnp.float32)
    stats = jnp.sum(stat_rows[:, :stat_count] + stat_rows[:, stat_count : 2 * stat_count], 0)
    stats = stats.reshape(env_count, step_count, experts + 1)
    squares, logits = stats[..., 0], stats[..., 1:]
    root_mean = jnp.sqrt(squares / width + 1e-05)[..., None]
    logits = logits / root_mean
    expert_ids = lax.broadcasted_iota(jnp.int32, (1, 1, 1, experts), 3)
    picked_logits = jnp.sum(
        jnp.where(routes[..., None] == expert_ids, logits[:, :, None, :], 0.0), -1
    )
    first_gate = 1.0 / (1.0 + jnp.exp(picked_logits[..., 1] - picked_logits[..., 0]))
    second_gate = 1.0 - first_gate

    rows = gathered.reshape(group_count, tensor_count, block_rows + 2, slice_width)
    gains = rows[0, :, block_rows].astype(jnp.float32)
    wide = rows.astype(jnp.float32)
    slot_scale = jnp.sqrt(jnp.sum(wide * wide, axis=(1, 3)) / width + 1e-05)[..., None]
    scaled_rows = (wide * gains[None, :, None, :]).astype(jnp.bfloat16)

    def expert_in(weights):
        split = weights.reshape(tensor_count, slice_width, hidden_local)
        sums = jnp.einsum("gtrd,tdf->grf", scaled_rows, split, preferred_element_type=jnp.float32)
        sums = (sums / slot_scale)[:, :block_rows]
        return sums.reshape(local_experts, group_count, owner_count, CAP, hidden_local)

    gate_sums = expert_in(w_gate)
    up_sums = expert_in(w_up)
    hidden = (jax.nn.silu(gate_sums) * up_sums).astype(jnp.bfloat16)
    down_split = w_down.reshape(local_experts, hidden_local, tensor_count, slice_width)
    owner_half = owner_count // 2
    group_half = group_count // 2
    tensor_half = tensor_count // 2

    def down(rows, columns, spec):
        return jnp.einsum(spec, rows, columns, preferred_element_type=jnp.float32)

    z_rows = hidden[:, :, :owner_half]
    y_rows = hidden[:, :, owner_half:]
    z_first = both_ways(
        down(z_rows[:, :group_half], down_split, "jgacf,jftd->tgajcd"),
        down(z_rows[:, group_half:], down_split, "jgacf,jftd->tgajcd"),
        "tp",
        0,
    )
    y_first = both_ways(
        down(y_rows, down_split[:, :, :tensor_half], "jgacf,jftd->gtajcd"),
        down(y_rows, down_split[:, :, tensor_half:], "jgacf,jftd->gtajcd"),
        "grp",
        0,
    )
    z_done = lax.psum_scatter(z_first.astype(jnp.bfloat16), "grp", scatter_dimension=0, tiled=True)
    z_done = z_done[0].astype(jnp.float32)
    y_done = exchange_sum(y_first, "tp")
    summed = jnp.concatenate([z_done, y_done], axis=0)
    returned = lax.all_to_all(
        summed.astype(jnp.bfloat16), "ex", split_axis=0, concat_axis=0, tiled=True
    )
    returned = returned.reshape(experts * CAP, slice_width)
    picked_rows = jnp.einsum("rks,sd->rkd", placed, returned, preferred_element_type=jnp.float32)
    picked_rows = picked_rows.reshape(env_count, step_count, topk, slice_width)
    expert_mix = (
        first_gate[..., None] * picked_rows[:, :, 0] + second_gate[..., None] * picked_rows[:, :, 1]
    )
    return (attended, expert_mix.astype(jnp.bfloat16))


def solution(mesh):
    return jax.shard_map(
        per_device,
        mesh=mesh,
        in_specs=(
            P(("grp", "ex"), None, "tp"),
            P(("grp", "ex"), None, "tp"),
            P(("grp", "ex"), None, "tp"),
            P(("grp", "ex"), None, "tp"),
            P(("grp", "ex"), "tp", None, None),
            P(("grp", "ex"), "tp", None, None),
            P(("grp", "ex")),
            P("tp"),
            P("tp", None),
            P(("grp", "ex"), None, None),
            P("ex", None, ("grp", "tp")),
            P("ex", None, ("grp", "tp")),
            P("ex", ("grp", "tp"), None),
        ),
        out_specs=(P(("grp", "ex"), None, "tp"), P(("grp", "ex"), None, "tp")),
        check_vma=False,
    )
```

```python
import jax
import jax.numpy as jnp
from jax import lax
from jax.sharding import PartitionSpec as P

CAP = 16


def attend(query_new, key_new, value_new, key_cache, value_cache, lengths):
    env_count, step_count, feature_count = query_new.shape
    kv_count = key_cache.shape[1]
    context = key_cache.shape[2]
    head_dim = key_cache.shape[3]
    group_size = feature_count // (kv_count * head_dim)
    queries = query_new.reshape(env_count, step_count, kv_count, group_size, head_dim)
    keys_now = key_new.reshape(env_count, step_count, kv_count, head_dim)
    values_now = value_new.reshape(env_count, step_count, kv_count, head_dim)
    score_scale = head_dim ** (-0.5)
    cached = (
        jnp.einsum("eskgd,ekcd->eskgc", queries, key_cache, preferred_element_type=jnp.float32)
        * score_scale
    )
    fresh_scores = (
        jnp.einsum("eskgd,etkd->eskgt", queries, keys_now, preferred_element_type=jnp.float32)
        * score_scale
    )
    valid_mask = (lax.broadcasted_iota(jnp.int32, (env_count, context), 1) < lengths[:, None])[
        :, None, None, None, :
    ]
    causal = (
        lax.broadcasted_iota(jnp.int32, (step_count, step_count), 1)
        <= lax.broadcasted_iota(jnp.int32, (step_count, step_count), 0)
    )[None, :, None, None, :]
    cached = jnp.where(valid_mask, cached, -1e30)
    fresh_scores = jnp.where(causal, fresh_scores, -1e30)
    row_top = jnp.maximum(jnp.max(cached, -1), jnp.max(fresh_scores, -1))[..., None]
    weight_cached = jnp.where(valid_mask, jnp.exp(cached - row_top), 0.0)
    weight_fresh = jnp.where(causal, jnp.exp(fresh_scores - row_top), 0.0)
    row_total = (jnp.sum(weight_cached, -1) + jnp.sum(weight_fresh, -1))[..., None]
    probs_cached = (weight_cached / row_total).astype(jnp.bfloat16)
    probs_fresh = (weight_fresh / row_total).astype(jnp.bfloat16)
    heads_out = jnp.einsum(
        "eskgc,ekcd->eskgd", probs_cached, value_cache, preferred_element_type=jnp.float32
    )
    heads_out = heads_out + jnp.einsum(
        "eskgt,etkd->eskgd", probs_fresh, values_now, preferred_element_type=jnp.float32
    )
    return heads_out.reshape(env_count, step_count, feature_count)


def ring_reduce_scatter(parts, axis, count, direction):
    me = lax.axis_index(axis)
    pairs = [(j, (j + direction) % count) for j in range(count)]

    def own(offset):
        chunk = (me - direction * offset) % count
        return lax.dynamic_index_in_dim(parts, chunk, 0, keepdims=False)

    total = own(1)
    for step in range(count - 1):
        arrived = lax.ppermute(total.astype(jnp.bfloat16), axis, pairs)
        total = arrived.astype(jnp.float32) + own(step + 2)
    return total


def both_ways(forward, backward, axis, joined):
    count = lax.axis_size(axis)
    return jnp.concatenate(
        [
            ring_reduce_scatter(forward, axis, count, 1),
            ring_reduce_scatter(backward, axis, count, -1),
        ],
        axis=joined,
    )


def exchange_sum(parts, axis):
    moved = lax.all_to_all(parts.astype(jnp.bfloat16), axis, 0, 0, tiled=True)
    return jnp.sum(moved.astype(jnp.float32), axis=0)


def per_device(
    residual,
    query_new,
    key_new,
    value_new,
    key_cache,
    value_cache,
    lengths,
    norm_gain,
    router,
    routes,
    w_gate,
    w_up,
    w_down,
):
    env_count, step_count, slice_width = residual.shape
    local_experts, width, hidden_local = w_gate.shape
    experts = router.shape[1]
    topk = routes.shape[2]
    group_count = lax.axis_size("grp")
    tensor_count = lax.axis_size("tp")
    owner_count = lax.axis_size("ex")
    row_count = env_count * step_count
    state = residual.astype(jnp.float32) + attend(
        query_new, key_new, value_new, key_cache, value_cache, lengths
    )
    attended = state.astype(jnp.bfloat16)
    squares = jnp.sum(state * state, -1)
    scaled = state * norm_gain.astype(jnp.float32)
    partial_logits = jnp.einsum("esd,dx->esx", scaled, router, precision=lax.Precision.HIGHEST)
    stats = jnp.concatenate([squares[..., None], partial_logits], axis=-1)
    stats_high = stats.astype(jnp.bfloat16)
    stats_low = (stats - stats_high.astype(jnp.float32)).astype(jnp.bfloat16)
    stat_count = stats.size
    extras = jnp.zeros((2, slice_width), jnp.bfloat16)
    extras = extras.at[0].set(norm_gain)
    extras = extras.at[1, :stat_count].set(stats_high.reshape(stat_count))
    extras = extras.at[1, stat_count : 2 * stat_count].set(stats_low.reshape(stat_count))
    flat_routes = routes.reshape(row_count * topk)
    expert_hits = (flat_routes[:, None] == lax.broadcasted_iota(jnp.int32, (1, experts), 1)).astype(
        jnp.int32
    )
    earlier = jnp.cumsum(expert_hits, axis=0) - expert_hits
    slot_ids = jnp.sum(earlier * expert_hits, axis=1)
    targets = flat_routes * CAP + slot_ids
    slot_table = lax.broadcasted_iota(jnp.int32, (1, experts * CAP), 1)
    placed = (
        (targets[:, None] == slot_table)
        .astype(jnp.bfloat16)
        .reshape(row_count, topk, experts * CAP)
    )
    sender = jnp.sum(placed, axis=1)
    packed = jnp.einsum(
        "rs,rd->sd",
        sender,
        attended.reshape(row_count, slice_width),
        preferred_element_type=jnp.float32,
    )
    outgoing = packed.astype(jnp.bfloat16).reshape(experts, CAP, slice_width)
    received = lax.all_to_all(outgoing, "ex", split_axis=0, concat_axis=0, tiled=True)
    block_rows = owner_count * local_experts * CAP
    payload = jnp.concatenate([received.reshape(block_rows, slice_width), extras], axis=0)
    gathered = lax.all_gather(payload[None], ("grp", "tp"), axis=0, tiled=True)
    stat_rows = gathered[:, block_rows + 1].reshape(group_count, tensor_count, slice_width)
    stat_rows = lax.dynamic_index_in_dim(stat_rows, lax.axis_index("grp"), 0, keepdims=False)
    stat_rows = stat_rows.astype(jnp.float32)
    stats = jnp.sum(stat_rows[:, :stat_count] + stat_rows[:, stat_count : 2 * stat_count], 0)
    stats = stats.reshape(env_count, step_count, experts + 1)
    squares, logits = stats[..., 0], stats[..., 1:]
    root_mean = jnp.sqrt(squares / width + 1e-05)[..., None]
    logits = logits / root_mean
    expert_ids = lax.broadcasted_iota(jnp.int32, (1, 1, 1, experts), 3)
    picked_logits = jnp.sum(
        jnp.where(routes[..., None] == expert_ids, logits[:, :, None, :], 0.0), -1
    )
    first_gate = 1.0 / (1.0 + jnp.exp(picked_logits[..., 1] - picked_logits[..., 0]))
    second_gate = 1.0 - first_gate

    rows = gathered.reshape(group_count, tensor_count, block_rows + 2, slice_width)
    gains = rows[0, :, block_rows].astype(jnp.float32)
    wide = rows.astype(jnp.float32)
    slot_scale = jnp.sqrt(jnp.sum(wide * wide, axis=(1, 3)) / width + 1e-05)[..., None]
    scaled_rows = (wide * gains[None, :, None, :]).astype(jnp.bfloat16)

    def expert_in(weights):
        split = weights.reshape(tensor_count, slice_width, hidden_local)
        sums = jnp.einsum("gtrd,tdf->grf", scaled_rows, split, preferred_element_type=jnp.float32)
        sums = (sums / slot_scale)[:, :block_rows]
        return sums.reshape(local_experts, group_count, owner_count, CAP, hidden_local)

    gate_sums = expert_in(w_gate)
    up_sums = expert_in(w_up)
    hidden = (jax.nn.silu(gate_sums) * up_sums).astype(jnp.bfloat16)
    down_split = w_down.reshape(local_experts, hidden_local, tensor_count, slice_width)
    owner_half = owner_count // 2
    group_half = group_count // 2

    def down(rows, columns, spec):
        return jnp.einsum(spec, rows, columns, preferred_element_type=jnp.float32)

    z_rows = hidden[:, :, :owner_half]
    y_rows = hidden[:, :, owner_half:]
    z_first = both_ways(
        down(z_rows[:, :group_half], down_split, "jgacf,jftd->tgajcd"),
        down(z_rows[:, group_half:], down_split, "jgacf,jftd->tgajcd"),
        "tp",
        0,
    )
    y_first = lax.psum_scatter(
        down(y_rows, down_split, "jgacf,jftd->gtajcd").astype(jnp.bfloat16),
        "grp",
        scatter_dimension=0,
        tiled=True,
    )
    y_first = y_first[0].astype(jnp.float32)
    z_done = lax.psum_scatter(z_first.astype(jnp.bfloat16), "grp", scatter_dimension=0, tiled=True)
    z_done = z_done[0].astype(jnp.float32)
    y_done = exchange_sum(y_first, "tp")
    summed = jnp.concatenate([z_done, y_done], axis=0)
    returned = lax.all_to_all(
        summed.astype(jnp.bfloat16), "ex", split_axis=0, concat_axis=0, tiled=True
    )
    returned = returned.reshape(experts * CAP, slice_width)
    picked_rows = jnp.einsum("rks,sd->rkd", placed, returned, preferred_element_type=jnp.float32)
    picked_rows = picked_rows.reshape(env_count, step_count, topk, slice_width)
    expert_mix = (
        first_gate[..., None] * picked_rows[:, :, 0] + second_gate[..., None] * picked_rows[:, :, 1]
    )
    return (attended, expert_mix.astype(jnp.bfloat16))


def solution(mesh):
    return jax.shard_map(
        per_device,
        mesh=mesh,
        in_specs=(
            P(("grp", "ex"), None, "tp"),
            P(("grp", "ex"), None, "tp"),
            P(("grp", "ex"), None, "tp"),
            P(("grp", "ex"), None, "tp"),
            P(("grp", "ex"), "tp", None, None),
            P(("grp", "ex"), "tp", None, None),
            P(("grp", "ex")),
            P("tp"),
            P("tp", None),
            P(("grp", "ex"), None, None),
            P("ex", None, ("grp", "tp")),
            P("ex", None, ("grp", "tp")),
            P("ex", ("grp", "tp"), None),
        ),
        out_specs=(P(("grp", "ex"), None, "tp"), P(("grp", "ex"), None, "tp")),
        check_vma=False,
    )
```

```python
import jax
import jax.numpy as jnp
from jax import lax
from jax.sharding import PartitionSpec as P

CAP = 16


def attend(query_new, key_new, value_new, key_cache, value_cache, lengths):
    env_count, step_count, feature_count = query_new.shape
    kv_count = key_cache.shape[1]
    context = key_cache.shape[2]
    head_dim = key_cache.shape[3]
    group_size = feature_count // (kv_count * head_dim)
    queries = query_new.reshape(env_count, step_count, kv_count, group_size, head_dim)
    keys_now = key_new.reshape(env_count, step_count, kv_count, head_dim)
    values_now = value_new.reshape(env_count, step_count, kv_count, head_dim)
    score_scale = head_dim ** (-0.5)
    cached = (
        jnp.einsum("eskgd,ekcd->eskgc", queries, key_cache, preferred_element_type=jnp.float32)
        * score_scale
    )
    fresh_scores = (
        jnp.einsum("eskgd,etkd->eskgt", queries, keys_now, preferred_element_type=jnp.float32)
        * score_scale
    )
    valid_mask = (lax.broadcasted_iota(jnp.int32, (env_count, context), 1) < lengths[:, None])[
        :, None, None, None, :
    ]
    causal = (
        lax.broadcasted_iota(jnp.int32, (step_count, step_count), 1)
        <= lax.broadcasted_iota(jnp.int32, (step_count, step_count), 0)
    )[None, :, None, None, :]
    cached = jnp.where(valid_mask, cached, -1e30)
    fresh_scores = jnp.where(causal, fresh_scores, -1e30)
    row_top = jnp.maximum(jnp.max(cached, -1), jnp.max(fresh_scores, -1))[..., None]
    weight_cached = jnp.where(valid_mask, jnp.exp(cached - row_top), 0.0)
    weight_fresh = jnp.where(causal, jnp.exp(fresh_scores - row_top), 0.0)
    row_total = (jnp.sum(weight_cached, -1) + jnp.sum(weight_fresh, -1))[..., None]
    probs_cached = (weight_cached / row_total).astype(jnp.bfloat16)
    probs_fresh = (weight_fresh / row_total).astype(jnp.bfloat16)
    heads_out = jnp.einsum(
        "eskgc,ekcd->eskgd", probs_cached, value_cache, preferred_element_type=jnp.float32
    )
    heads_out = heads_out + jnp.einsum(
        "eskgt,etkd->eskgd", probs_fresh, values_now, preferred_element_type=jnp.float32
    )
    return heads_out.reshape(env_count, step_count, feature_count)


def ring_reduce_scatter(parts, axis, count, direction):
    me = lax.axis_index(axis)
    pairs = [(j, (j + direction) % count) for j in range(count)]

    def own(offset):
        chunk = (me - direction * offset) % count
        return lax.dynamic_index_in_dim(parts, chunk, 0, keepdims=False)

    total = own(1)
    for step in range(count - 1):
        arrived = lax.ppermute(total.astype(jnp.bfloat16), axis, pairs)
        total = arrived.astype(jnp.float32) + own(step + 2)
    return total


def both_ways(forward, backward, axis, joined):
    count = lax.axis_size(axis)
    return jnp.concatenate(
        [
            ring_reduce_scatter(forward, axis, count, 1),
            ring_reduce_scatter(backward, axis, count, -1),
        ],
        axis=joined,
    )


def exchange_sum(parts, axis):
    moved = lax.all_to_all(parts.astype(jnp.bfloat16), axis, 0, 0, tiled=True)
    return jnp.sum(moved.astype(jnp.float32), axis=0)


def per_device(
    residual,
    query_new,
    key_new,
    value_new,
    key_cache,
    value_cache,
    lengths,
    norm_gain,
    router,
    routes,
    w_gate,
    w_up,
    w_down,
):
    env_count, step_count, slice_width = residual.shape
    local_experts, width, hidden_local = w_gate.shape
    experts = router.shape[1]
    topk = routes.shape[2]
    group_count = lax.axis_size("grp")
    tensor_count = lax.axis_size("tp")
    owner_count = lax.axis_size("ex")
    row_count = env_count * step_count
    state = residual.astype(jnp.float32) + attend(
        query_new, key_new, value_new, key_cache, value_cache, lengths
    )
    attended = state.astype(jnp.bfloat16)
    squares = jnp.sum(state * state, -1)
    scaled = state * norm_gain.astype(jnp.float32)
    partial_logits = jnp.einsum("esd,dx->esx", scaled, router, precision=lax.Precision.HIGHEST)
    stats = jnp.concatenate([squares[..., None], partial_logits], axis=-1)
    stats_high = stats.astype(jnp.bfloat16)
    stats_low = (stats - stats_high.astype(jnp.float32)).astype(jnp.bfloat16)
    stat_count = stats.size
    extras = jnp.zeros((2, slice_width), jnp.bfloat16)
    extras = extras.at[0].set(norm_gain)
    extras = extras.at[1, :stat_count].set(stats_high.reshape(stat_count))
    extras = extras.at[1, stat_count : 2 * stat_count].set(stats_low.reshape(stat_count))
    flat_routes = routes.reshape(row_count * topk)
    expert_hits = (flat_routes[:, None] == lax.broadcasted_iota(jnp.int32, (1, experts), 1)).astype(
        jnp.int32
    )
    earlier = jnp.cumsum(expert_hits, axis=0) - expert_hits
    slot_ids = jnp.sum(earlier * expert_hits, axis=1)
    targets = flat_routes * CAP + slot_ids
    slot_table = lax.broadcasted_iota(jnp.int32, (1, experts * CAP), 1)
    placed = (
        (targets[:, None] == slot_table)
        .astype(jnp.bfloat16)
        .reshape(row_count, topk, experts * CAP)
    )
    sender = jnp.sum(placed, axis=1)
    packed = jnp.einsum(
        "rs,rd->sd",
        sender,
        attended.reshape(row_count, slice_width),
        preferred_element_type=jnp.float32,
    )
    outgoing = packed.astype(jnp.bfloat16).reshape(experts, CAP, slice_width)
    received = lax.all_to_all(outgoing, "ex", split_axis=0, concat_axis=0, tiled=True)
    block_rows = owner_count * local_experts * CAP
    payload = jnp.concatenate([received.reshape(block_rows, slice_width), extras], axis=0)
    gathered = lax.all_gather(payload[None], ("grp", "tp"), axis=0, tiled=True)
    stat_rows = gathered[:, block_rows + 1].reshape(group_count, tensor_count, slice_width)
    stat_rows = lax.dynamic_index_in_dim(stat_rows, lax.axis_index("grp"), 0, keepdims=False)
    stat_rows = stat_rows.astype(jnp.float32)
    stats = jnp.sum(stat_rows[:, :stat_count] + stat_rows[:, stat_count : 2 * stat_count], 0)
    stats = stats.reshape(env_count, step_count, experts + 1)
    squares, logits = stats[..., 0], stats[..., 1:]
    root_mean = jnp.sqrt(squares / width + 1e-05)[..., None]
    logits = logits / root_mean
    expert_ids = lax.broadcasted_iota(jnp.int32, (1, 1, 1, experts), 3)
    picked_logits = jnp.sum(
        jnp.where(routes[..., None] == expert_ids, logits[:, :, None, :], 0.0), -1
    )
    first_gate = 1.0 / (1.0 + jnp.exp(picked_logits[..., 1] - picked_logits[..., 0]))
    second_gate = 1.0 - first_gate

    rows = gathered.reshape(group_count, tensor_count, block_rows + 2, slice_width)
    gains = rows[0, :, block_rows].astype(jnp.float32)
    wide = rows.astype(jnp.float32)
    slot_scale = jnp.sqrt(jnp.sum(wide * wide, axis=(1, 3)) / width + 1e-05)[..., None]
    scaled_rows = (wide * gains[None, :, None, :]).astype(jnp.bfloat16)

    def expert_in(weights):
        split = weights.reshape(tensor_count, slice_width, hidden_local)
        sums = jnp.einsum("gtrd,tdf->grf", scaled_rows, split, preferred_element_type=jnp.float32)
        sums = (sums / slot_scale)[:, :block_rows]
        return sums.reshape(local_experts, group_count, owner_count, CAP, hidden_local)

    gate_sums = expert_in(w_gate)
    up_sums = expert_in(w_up)
    hidden = (jax.nn.silu(gate_sums) * up_sums).astype(jnp.bfloat16)
    down_split = w_down.reshape(local_experts, hidden_local, tensor_count, slice_width)
    owner_half = (owner_count * 3) // 8
    group_half = group_count // 2
    tensor_half = tensor_count // 2

    def down(rows, columns, spec):
        return jnp.einsum(spec, rows, columns, preferred_element_type=jnp.float32)

    z_rows = hidden[:, :, :owner_half]
    y_rows = hidden[:, :, owner_half:]
    z_first = both_ways(
        down(z_rows[:, :group_half], down_split, "jgacf,jftd->tgajcd"),
        down(z_rows[:, group_half:], down_split, "jgacf,jftd->tgajcd"),
        "tp",
        0,
    )
    y_first = both_ways(
        down(y_rows, down_split[:, :, :tensor_half], "jgacf,jftd->gtajcd"),
        down(y_rows, down_split[:, :, tensor_half:], "jgacf,jftd->gtajcd"),
        "grp",
        0,
    )
    z_done = lax.psum_scatter(z_first.astype(jnp.bfloat16), "grp", scatter_dimension=0, tiled=True)
    z_done = z_done[0].astype(jnp.float32)
    y_done = exchange_sum(y_first, "tp")
    summed = jnp.concatenate([z_done, y_done], axis=0)
    returned = lax.all_to_all(
        summed.astype(jnp.bfloat16), "ex", split_axis=0, concat_axis=0, tiled=True
    )
    returned = returned.reshape(experts * CAP, slice_width)
    picked_rows = jnp.einsum("rks,sd->rkd", placed, returned, preferred_element_type=jnp.float32)
    picked_rows = picked_rows.reshape(env_count, step_count, topk, slice_width)
    expert_mix = (
        first_gate[..., None] * picked_rows[:, :, 0] + second_gate[..., None] * picked_rows[:, :, 1]
    )
    return (attended, expert_mix.astype(jnp.bfloat16))


def solution(mesh):
    return jax.shard_map(
        per_device,
        mesh=mesh,
        in_specs=(
            P(("grp", "ex"), None, "tp"),
            P(("grp", "ex"), None, "tp"),
            P(("grp", "ex"), None, "tp"),
            P(("grp", "ex"), None, "tp"),
            P(("grp", "ex"), "tp", None, None),
            P(("grp", "ex"), "tp", None, None),
            P(("grp", "ex")),
            P("tp"),
            P("tp", None),
            P(("grp", "ex"), None, None),
            P("ex", None, ("grp", "tp")),
            P("ex", None, ("grp", "tp")),
            P("ex", ("grp", "tp"), None),
        ),
        out_specs=(P(("grp", "ex"), None, "tp"), P(("grp", "ex"), None, "tp")),
        check_vma=False,
    )
```

```python
import jax
import jax.numpy as jnp
from jax import lax
from jax.sharding import PartitionSpec as P

CAP = 16


def attend(query_new, key_new, value_new, key_cache, value_cache, lengths):
    env_count, step_count, feature_count = query_new.shape
    kv_count = key_cache.shape[1]
    context = key_cache.shape[2]
    head_dim = key_cache.shape[3]
    group_size = feature_count // (kv_count * head_dim)
    queries = query_new.reshape(env_count, step_count, kv_count, group_size, head_dim)
    keys_now = key_new.reshape(env_count, step_count, kv_count, head_dim)
    values_now = value_new.reshape(env_count, step_count, kv_count, head_dim)
    score_scale = head_dim ** (-0.5)
    cached = (
        jnp.einsum("eskgd,ekcd->eskgc", queries, key_cache, preferred_element_type=jnp.float32)
        * score_scale
    )
    fresh_scores = (
        jnp.einsum("eskgd,etkd->eskgt", queries, keys_now, preferred_element_type=jnp.float32)
        * score_scale
    )
    valid_mask = (lax.broadcasted_iota(jnp.int32, (env_count, context), 1) < lengths[:, None])[
        :, None, None, None, :
    ]
    causal = (
        lax.broadcasted_iota(jnp.int32, (step_count, step_count), 1)
        <= lax.broadcasted_iota(jnp.int32, (step_count, step_count), 0)
    )[None, :, None, None, :]
    cached = jnp.where(valid_mask, cached, -1e30)
    fresh_scores = jnp.where(causal, fresh_scores, -1e30)
    row_top = jnp.maximum(jnp.max(cached, -1), jnp.max(fresh_scores, -1))[..., None]
    weight_cached = jnp.where(valid_mask, jnp.exp(cached - row_top), 0.0)
    weight_fresh = jnp.where(causal, jnp.exp(fresh_scores - row_top), 0.0)
    row_total = (jnp.sum(weight_cached, -1) + jnp.sum(weight_fresh, -1))[..., None]
    probs_cached = (weight_cached / row_total).astype(jnp.bfloat16)
    probs_fresh = (weight_fresh / row_total).astype(jnp.bfloat16)
    heads_out = jnp.einsum(
        "eskgc,ekcd->eskgd", probs_cached, value_cache, preferred_element_type=jnp.float32
    )
    heads_out = heads_out + jnp.einsum(
        "eskgt,etkd->eskgd", probs_fresh, values_now, preferred_element_type=jnp.float32
    )
    return heads_out.reshape(env_count, step_count, feature_count)


def ring_reduce_scatter(parts, axis, count, direction):
    me = lax.axis_index(axis)
    pairs = [(j, (j + direction) % count) for j in range(count)]

    def own(offset):
        chunk = (me - direction * offset) % count
        return lax.dynamic_index_in_dim(parts, chunk, 0, keepdims=False)

    total = own(1)
    for step in range(count - 1):
        arrived = lax.ppermute(total.astype(jnp.bfloat16), axis, pairs)
        total = arrived.astype(jnp.float32) + own(step + 2)
    return total


def both_ways(forward, backward, axis, joined):
    count = lax.axis_size(axis)
    return jnp.concatenate(
        [
            ring_reduce_scatter(forward, axis, count, 1),
            ring_reduce_scatter(backward, axis, count, -1),
        ],
        axis=joined,
    )


def exchange_sum(parts, axis):
    moved = lax.all_to_all(parts.astype(jnp.bfloat16), axis, 0, 0, tiled=True)
    return jnp.sum(moved.astype(jnp.float32), axis=0)


def per_device(
    residual,
    query_new,
    key_new,
    value_new,
    key_cache,
    value_cache,
    lengths,
    norm_gain,
    router,
    routes,
    w_gate,
    w_up,
    w_down,
):
    env_count, step_count, slice_width = residual.shape
    local_experts, width, hidden_local = w_gate.shape
    experts = router.shape[1]
    topk = routes.shape[2]
    group_count = lax.axis_size("grp")
    tensor_count = lax.axis_size("tp")
    owner_count = lax.axis_size("ex")
    row_count = env_count * step_count
    state = residual.astype(jnp.float32) + attend(
        query_new, key_new, value_new, key_cache, value_cache, lengths
    )
    attended = state.astype(jnp.bfloat16)
    squares = jnp.sum(state * state, -1)
    scaled = state * norm_gain.astype(jnp.float32)
    partial_logits = jnp.einsum("esd,dx->esx", scaled, router, precision=lax.Precision.HIGHEST)
    stats = jnp.concatenate([squares[..., None], partial_logits], axis=-1)
    stats_high = stats.astype(jnp.bfloat16)
    stats_low = (stats - stats_high.astype(jnp.float32)).astype(jnp.bfloat16)
    stat_count = stats.size
    extras = jnp.zeros((2, slice_width), jnp.bfloat16)
    extras = extras.at[0].set(norm_gain)
    extras = extras.at[1, :stat_count].set(stats_high.reshape(stat_count))
    extras = extras.at[1, stat_count : 2 * stat_count].set(stats_low.reshape(stat_count))
    flat_routes = routes.reshape(row_count * topk)
    expert_hits = (flat_routes[:, None] == lax.broadcasted_iota(jnp.int32, (1, experts), 1)).astype(
        jnp.int32
    )
    earlier = jnp.cumsum(expert_hits, axis=0) - expert_hits
    slot_ids = jnp.sum(earlier * expert_hits, axis=1)
    targets = flat_routes * CAP + slot_ids
    slot_table = lax.broadcasted_iota(jnp.int32, (1, experts * CAP), 1)
    placed = (
        (targets[:, None] == slot_table)
        .astype(jnp.bfloat16)
        .reshape(row_count, topk, experts * CAP)
    )
    sender = jnp.sum(placed, axis=1)
    packed = jnp.einsum(
        "rs,rd->sd",
        sender,
        attended.reshape(row_count, slice_width),
        preferred_element_type=jnp.float32,
    )
    outgoing = packed.astype(jnp.bfloat16).reshape(experts, CAP, slice_width)
    received = lax.all_to_all(outgoing, "ex", split_axis=0, concat_axis=0, tiled=True)
    block_rows = owner_count * local_experts * CAP
    payload = jnp.concatenate([received.reshape(block_rows, slice_width), extras], axis=0)
    gathered = lax.all_gather(payload[None], ("grp", "tp"), axis=0, tiled=True)
    stat_rows = gathered[:, block_rows + 1].reshape(group_count, tensor_count, slice_width)
    stat_rows = lax.dynamic_index_in_dim(stat_rows, lax.axis_index("grp"), 0, keepdims=False)
    stat_rows = stat_rows.astype(jnp.float32)
    stats = jnp.sum(stat_rows[:, :stat_count] + stat_rows[:, stat_count : 2 * stat_count], 0)
    stats = stats.reshape(env_count, step_count, experts + 1)
    squares, logits = stats[..., 0], stats[..., 1:]
    root_mean = jnp.sqrt(squares / width + 1e-05)[..., None]
    logits = logits / root_mean
    expert_ids = lax.broadcasted_iota(jnp.int32, (1, 1, 1, experts), 3)
    picked_logits = jnp.sum(
        jnp.where(routes[..., None] == expert_ids, logits[:, :, None, :], 0.0), -1
    )
    first_gate = 1.0 / (1.0 + jnp.exp(picked_logits[..., 1] - picked_logits[..., 0]))
    second_gate = 1.0 - first_gate

    rows = gathered.reshape(group_count, tensor_count, block_rows + 2, slice_width)
    gains = rows[0, :, block_rows].astype(jnp.float32)
    wide = rows.astype(jnp.float32)
    slot_scale = jnp.sqrt(jnp.sum(wide * wide, axis=(1, 3)) / width + 1e-05)[..., None]
    scaled_rows = (wide * gains[None, :, None, :]).astype(jnp.bfloat16)

    def expert_in(weights):
        split = weights.reshape(tensor_count, slice_width, hidden_local)
        sums = jnp.einsum("gtrd,tdf->grf", scaled_rows, split, preferred_element_type=jnp.float32)
        sums = (sums / slot_scale)[:, :block_rows]
        return sums.reshape(local_experts, group_count, owner_count, CAP, hidden_local)

    gate_sums = expert_in(w_gate)
    up_sums = expert_in(w_up)
    hidden = (jax.nn.silu(gate_sums) * up_sums).astype(jnp.bfloat16)
    down_split = w_down.reshape(local_experts, hidden_local, tensor_count, slice_width)
    owner_half = (owner_count * 5) // 8
    group_half = group_count // 2
    tensor_half = tensor_count // 2

    def down(rows, columns, spec):
        return jnp.einsum(spec, rows, columns, preferred_element_type=jnp.float32)

    z_rows = hidden[:, :, :owner_half]
    y_rows = hidden[:, :, owner_half:]
    z_first = both_ways(
        down(z_rows[:, :group_half], down_split, "jgacf,jftd->tgajcd"),
        down(z_rows[:, group_half:], down_split, "jgacf,jftd->tgajcd"),
        "tp",
        0,
    )
    y_first = both_ways(
        down(y_rows, down_split[:, :, :tensor_half], "jgacf,jftd->gtajcd"),
        down(y_rows, down_split[:, :, tensor_half:], "jgacf,jftd->gtajcd"),
        "grp",
        0,
    )
    z_done = lax.psum_scatter(z_first.astype(jnp.bfloat16), "grp", scatter_dimension=0, tiled=True)
    z_done = z_done[0].astype(jnp.float32)
    y_done = exchange_sum(y_first, "tp")
    summed = jnp.concatenate([z_done, y_done], axis=0)
    returned = lax.all_to_all(
        summed.astype(jnp.bfloat16), "ex", split_axis=0, concat_axis=0, tiled=True
    )
    returned = returned.reshape(experts * CAP, slice_width)
    picked_rows = jnp.einsum("rks,sd->rkd", placed, returned, preferred_element_type=jnp.float32)
    picked_rows = picked_rows.reshape(env_count, step_count, topk, slice_width)
    expert_mix = (
        first_gate[..., None] * picked_rows[:, :, 0] + second_gate[..., None] * picked_rows[:, :, 1]
    )
    return (attended, expert_mix.astype(jnp.bfloat16))


def solution(mesh):
    return jax.shard_map(
        per_device,
        mesh=mesh,
        in_specs=(
            P(("grp", "ex"), None, "tp"),
            P(("grp", "ex"), None, "tp"),
            P(("grp", "ex"), None, "tp"),
            P(("grp", "ex"), None, "tp"),
            P(("grp", "ex"), "tp", None, None),
            P(("grp", "ex"), "tp", None, None),
            P(("grp", "ex")),
            P("tp"),
            P("tp", None),
            P(("grp", "ex"), None, None),
            P("ex", None, ("grp", "tp")),
            P("ex", None, ("grp", "tp")),
            P("ex", ("grp", "tp"), None),
        ),
        out_specs=(P(("grp", "ex"), None, "tp"), P(("grp", "ex"), None, "tp")),
        check_vma=False,
    )
```
